128 devices in a mesh: req: 32 (over x, z, core), mlp: 4 (over y).
Axes of the slice: x: 4, y: 4, z: 4, core: 2. Of those that a mesh axis runs over, the one named last changes fastest.
Arguments:
- hidden_in: bfloat16 [4096, 4096], P('req'), may hold values from -6 to 6
- attn_gain: bfloat16 [4096], replicated, may hold values from 0.5 to 1.5
- w_query: bfloat16 [4096, 2048], P(None, 'mlp'), may hold values from -0.09375 to 0.09375
- w_key: bfloat16 [4096, 512], P(None, 'mlp'), may hold values from -0.09375 to 0.09375
- w_value: bfloat16 [4096, 512], P(None, 'mlp'), may hold values from -0.09375 to 0.09375
- w_out: bfloat16 [2048, 4096], P('mlp'), may hold values from -0.125 to 0.125
- mlp_gain: bfloat16 [4096], replicated, may hold values from 0.5 to 1.5
- w_gate: bfloat16 [4096, 14336], P('mlp', 'req'), may hold values from -0.09375 to 0.09375
- w_up: bfloat16 [4096, 14336], P('mlp', 'req'), may hold values from -0.09375 to 0.09375
- w_down: bfloat16 [14336, 4096], P('req', 'mlp'), may hold values from -0.046875 to 0.046875
- prefix_kv: bfloat16 [65536, 2, 512], P('req', None, 'mlp'), may hold values from -512 to 512
- suffix_lengths: int32 [32, 4], P('req'), may hold values from 1 to 125, as said below
- prefix_owner: int32 [8, 4], replicated, may hold values from 0 to 3, each once within a row
Outputs:
- hidden_out: bfloat16 [4096, 4096], P('req', 'mlp')
- suffix_kv: bfloat16 [4096, 2, 512], P('req', None, 'mlp')
The draws below stay inside these ranges and needn't reach their ends.
Inputs may be any that keep to these rules, and one draw needn't show every extreme that they name: `suffix_lengths`: the lengths of one index of req sum to at most 128; in every draw some index sums to exactly 128. `prefix_owner`: each row is a permutation.
All inputs are finite; a program needn't handle non-finite values.
Results may differ from the reference program's by a relative error of at most 0.02.
The reference program's roundings to bfloat16 on the way count: a program that leaves them out, or rounds other values in their place, can miss the bound.
Values may be sent and summed in bfloat16 or wider, within the bound.
No kernel may reach another device: no remote copies, remote signals or barrier semaphores. Data moves between devices by JAX's collectives and lax.ppermute only.
A program may use at most 128 MiB of HBM per device.

```python
import math
import jax
import jax.numpy as jnp
from jax import lax

D = 4096
FF = 14336
HEAD_DIM = 128
HEADS_W = 16
KV_W = 4
PREFIX = 8192
GSPAN = 4
CAP = 128
REQ_DEV = 4
GROUPS = 8
PB = 2048
ROWS = 4096
N_REQ = 32


def draw_suffix_lengths(key, part):
    short_most = CAP // (2 * REQ_DEV)
    key_len, key_pick, key_slot = jax.random.split(key, 3)
    shorts = jax.random.randint(key_len, (N_REQ, REQ_DEV), 1, short_most + 1)
    order = jax.random.permutation(key_pick, N_REQ)
    heavy = max(1, N_REQ // 8)
    is_long = jnp.zeros((N_REQ,), jnp.int32).at[order[:heavy]].set(1)
    is_first = jnp.arange(N_REQ) == order[0]
    shorts = jnp.where(is_first[:, None], 1, shorts)
    where_long = jax.random.randint(key_slot, (N_REQ,), 0, REQ_DEV)
    at_slot = (jnp.arange(REQ_DEV)[None, :] == where_long[:, None]).astype(jnp.int32)
    others = jnp.sum(shorts * (1 - at_slot), axis=1)
    long_len = CAP - others
    result = jnp.where(is_long[:, None] * at_slot > 0, long_len[:, None], shorts)
    return result.astype(jnp.int32)


def draw_prefix_kv(key, part):
    key_k, key_v = jax.random.split(key, 2)
    block_rows = PREFIX // GSPAN
    rows_all = N_REQ * block_rows
    width = KV_W * HEAD_DIM
    shape = (rows_all, width)
    keys_raw = jnp.clip(2.5 * jax.random.normal(key_k, shape, jnp.float32), -15.0, 15.0)
    values_raw = jnp.clip(jax.random.normal(key_v, shape, jnp.float32), -6.0, 6.0)
    return jnp.stack([keys_raw, values_raw], axis=1).astype(jnp.bfloat16)


def block_levels(stream_key, dims, cuts, smallest, top_value):
    def one(axis_at, shards_of):
        heights = jax.random.uniform(jax.random.fold_in(jax.random.fold_in(stream_key, 6), axis_at), (shards_of,), jnp.float32, smallest / len(cuts), top_value / len(cuts))
        return jnp.repeat(jnp.exp(heights), dims[axis_at] // shards_of).reshape((-1,) + (1,) * (len(dims) - axis_at - 1))

    level = one(*cuts[0])
    for cut in cuts[1:]:
        level = level * one(*cut)
    return level


def bell_draw(rng, extent, spread, limit, shards=(), kind=jnp.bfloat16):
    array = jax.random.normal(rng, extent, jnp.float32) * spread
    if len(shards) > 0:
        array = block_levels(rng, extent, shards, -0.22, 0.18) * array
    return jnp.clip(array, min=-limit, max=limit).astype(kind)


def setup_inputs(seed: int = 0) -> dict:
    keys = jax.random.split(jax.random.key(seed), 14)
    hidden_in = bell_draw(keys[0], (ROWS, D), 1.0, 6.0, ((0, 32),))
    attn_gain = jnp.clip(1.0 + 0.1 * jax.random.normal(keys[1], (D,), jnp.float32), 0.5, 1.5).astype(jnp.bfloat16)
    w_query = bell_draw(keys[2], (D, HEADS_W * HEAD_DIM), D ** -0.5, 0.09375, ((1, 4),))
    w_key = bell_draw(keys[3], (D, KV_W * HEAD_DIM), D ** -0.5, 0.09375, ((1, 4),))
    w_value = bell_draw(keys[4], (D, KV_W * HEAD_DIM), D ** -0.5, 0.09375, ((1, 4),))
    w_out = bell_draw(keys[5], (HEADS_W * HEAD_DIM, D), (HEADS_W * HEAD_DIM) ** -0.5, 0.125, ((0, 4),))
    mlp_gain = jnp.clip(1.0 + 0.1 * jax.random.normal(keys[6], (D,), jnp.float32), 0.5, 1.5).astype(jnp.bfloat16)
    w_gate = bell_draw(keys[7], (D, FF), D ** -0.5, 0.09375, ((0, 4), (1, 32)))
    w_up = bell_draw(keys[8], (D, FF), D ** -0.5, 0.09375, ((0, 4), (1, 32)))
    w_down = bell_draw(keys[9], (FF, D), FF ** -0.5, 0.046875, ((0, 32), (1, 4)))
    prefix_kv = draw_prefix_kv(jax.random.fold_in(keys[13], 71), 0)
    suffix_lengths = draw_suffix_lengths(jax.random.fold_in(keys[13], 71), 0)
    prefix_owner = jax.vmap(lambda own: jax.random.permutation(own, GSPAN))(jax.random.split(keys[12], GROUPS)).reshape((GROUPS, GSPAN)).astype(jnp.int32)
    return dict(hidden_in=hidden_in, attn_gain=attn_gain, w_query=w_query, w_key=w_key, w_value=w_value, w_out=w_out, mlp_gain=mlp_gain, w_gate=w_gate, w_up=w_up, w_down=w_down, prefix_kv=prefix_kv, suffix_lengths=suffix_lengths, prefix_owner=prefix_owner)


rope_base = 500000.0
eps = 1e-05

def rope(values, positions):
    half = values.shape[-1] // 2
    freq = rope_base ** (-jnp.arange(half, dtype=jnp.float32) * 2.0 / values.shape[-1])
    angle = positions.astype(jnp.float32)[:, None] * freq[None, :]
    cosine = jnp.cos(angle)[:, None, :]
    sine = jnp.sin(angle)[:, None, :]
    former = values[..., :half]
    latter = values[..., half:]
    return jnp.concatenate([former * cosine - latter * sine, latter * cosine + former * sine], axis=-1)

def rms_norm(values, gain):
    return values * lax.rsqrt(lax.optimization_barrier(jnp.mean(values * values, axis=-1, keepdims=True)) + eps) * gain.astype(jnp.float32)

def slot_layout(lengths, slot_count):
    ends = jnp.cumsum(lengths)
    starts = ends - lengths
    slot_ids = jnp.arange(slot_count, dtype=jnp.int32)
    request_of = lax.optimization_barrier(jnp.sum((slot_ids[:, None] >= ends[None, :]).astype(jnp.int32), axis=1))
    picks = (request_of[:, None] == jnp.arange(lengths.shape[0], dtype=jnp.int32)[None, :]).astype(jnp.int32)
    start_of = lax.optimization_barrier(jnp.sum(picks * starts[None, :], axis=1))
    positions = PREFIX + slot_ids - start_of
    return (request_of, request_of < lengths.shape[0], positions)

def reference(hidden_in, attn_gain, w_query, w_key, w_value, w_out, mlp_gain, w_gate, w_up, w_down, prefix_kv, suffix_lengths, prefix_owner):
    group = HEADS_W // KV_W
    request_all, live_all, position_all = jax.vmap(lambda lengths: slot_layout(lengths, CAP))(suffix_lengths)
    live_flat = live_all.reshape(ROWS)
    position_flat = position_all.reshape(ROWS)
    hidden_f = hidden_in.astype(jnp.float32)
    normed = rms_norm(hidden_f, attn_gain).astype(jnp.bfloat16)
    query_rows = rope(jnp.dot(normed, w_query, preferred_element_type=jnp.float32).reshape(ROWS, HEADS_W, HEAD_DIM), position_flat).astype(jnp.bfloat16)
    key_rows = rope(jnp.dot(normed, w_key, preferred_element_type=jnp.float32).reshape(ROWS, KV_W, HEAD_DIM), position_flat).astype(jnp.bfloat16)
    value_rows = jnp.dot(normed, w_value, preferred_element_type=jnp.float32).astype(jnp.bfloat16).reshape(ROWS, KV_W, HEAD_DIM)
    stacked_kv = jnp.stack([key_rows.reshape(ROWS, KV_W * HEAD_DIM), value_rows.reshape(ROWS, KV_W * HEAD_DIM)], axis=1)
    suffix_kv = jnp.where(live_flat[:, None, None], stacked_kv, jnp.zeros_like(stacked_kv))
    stored = prefix_kv.reshape(GROUPS, GSPAN, PB, 2, KV_W * HEAD_DIM)
    ordered = jax.vmap(lambda blocks, owners: blocks[owners])(stored, prefix_owner)
    prefix_raw = ordered[:, :, :, 0].reshape(GROUPS, PREFIX, KV_W, HEAD_DIM).astype(jnp.float32)
    prefix_pos = jnp.arange(PREFIX, dtype=jnp.int32)
    prefix_keys = jax.vmap(lambda raw: rope(raw, prefix_pos))(prefix_raw).astype(jnp.bfloat16)
    prefix_values = ordered[:, :, :, 1].reshape(GROUPS, PREFIX, KV_W, HEAD_DIM)

    def attend(index):
        queries_here = lax.dynamic_slice_in_dim(query_rows, index * CAP, CAP, 0)
        keys_here = lax.dynamic_slice_in_dim(key_rows, index * CAP, CAP, 0)
        values_here = lax.dynamic_slice_in_dim(value_rows, index * CAP, CAP, 0)
        group_id = index // GSPAN
        keys_all = jnp.concatenate([lax.dynamic_index_in_dim(prefix_keys, group_id, 0, keepdims=False), keys_here], axis=0)
        values_all = jnp.concatenate([lax.dynamic_index_in_dim(prefix_values, group_id, 0, keepdims=False), values_here], axis=0)
        keys_rep = jnp.repeat(keys_all, group, axis=1)
        values_rep = jnp.repeat(values_all, group, axis=1)
        scores = jnp.einsum('qhd,khd->hqk', queries_here.astype(jnp.float32), keys_rep.astype(jnp.float32)) / math.sqrt(HEAD_DIM)
        request_here = lax.dynamic_index_in_dim(request_all, index, 0, keepdims=False)
        slot_ids = jnp.arange(CAP, dtype=jnp.int32)
        allowed = (request_here[:, None] == request_here[None, :]) & (slot_ids[None, :] <= slot_ids[:, None])
        mask = jnp.concatenate([jnp.ones((CAP, PREFIX), dtype=bool), allowed], axis=1)
        scores = jnp.where(mask[None], scores, -jnp.inf)
        peak = lax.optimization_barrier(jnp.max(scores, axis=-1, keepdims=True))
        weights = jnp.exp(scores - peak)
        weight_sum = lax.optimization_barrier(jnp.sum(weights, axis=-1))
        probs = weights.astype(jnp.bfloat16)
        mixed = jnp.einsum('hqk,khd->qhd', probs.astype(jnp.float32), values_rep.astype(jnp.float32))
        result = mixed / jnp.transpose(weight_sum)[:, :, None]
        return result.astype(jnp.bfloat16).reshape(CAP, HEADS_W * HEAD_DIM)
    attended = lax.map(attend, jnp.arange(N_REQ, dtype=jnp.int32)).reshape(ROWS, HEADS_W * HEAD_DIM)
    residual = (hidden_f + jnp.dot(attended, w_out, preferred_element_type=jnp.float32)).astype(jnp.bfloat16)
    normed_mlp = rms_norm(residual.astype(jnp.float32), mlp_gain).astype(jnp.bfloat16)
    gate = jnp.dot(normed_mlp, w_gate, preferred_element_type=jnp.float32)
    up_part = jnp.dot(normed_mlp, w_up, preferred_element_type=jnp.float32)
    act = (jax.nn.silu(gate) * up_part).astype(jnp.bfloat16)
    act_blocks = jnp.transpose(act.reshape(ROWS, N_REQ, FF // N_REQ), (1, 0, 2))
    down_blocks = w_down.reshape(N_REQ, FF // N_REQ, D)

    def add_block(carry, pair):
        term = jnp.dot(pair[0], pair[1], preferred_element_type=jnp.float32).astype(jnp.bfloat16)
        term = lax.optimization_barrier(term)
        return (carry + term.astype(jnp.float32), None)
    down, _ = lax.scan(add_block, jnp.zeros((ROWS, D), jnp.float32), (act_blocks, down_blocks))
    total = residual.astype(jnp.float32) + down
    hidden_out = jnp.where(live_flat[:, None], total, 0.0).astype(jnp.bfloat16)
    return (hidden_out, suffix_kv)
```

```python
import math

import jax
import jax.numpy as jnp
import numpy as np
from jax import lax
from jax.sharding import Mesh
from jax.sharding import PartitionSpec as P


HEAD_DIM = 128
PREFIX = 8192
GSPAN = 4

REQ = ("rx", "rc")

rope_base = 500000.0
eps = 1e-05


def from_partner(value, axis, stride, size):
    mask = 2**stride
    pairs = [(source, source ^ mask) for source in range(size)]
    return lax.ppermute(value, axis, pairs)


def rope(values, positions):
    half = values.shape[-1] // 2
    freq = rope_base ** (-jnp.arange(half, dtype=jnp.float32) * 2.0 / values.shape[-1])
    angle = positions.astype(jnp.float32)[:, None] * freq[None, :]
    cosine = jnp.cos(angle)[:, None, :]
    sine = jnp.sin(angle)[:, None, :]
    former = values[..., :half]
    latter = values[..., half:]
    return jnp.concatenate(
        [former * cosine - latter * sine, latter * cosine + former * sine], axis=-1
    )


def rms_norm(values, gain):
    return (
        values
        * lax.rsqrt(jnp.mean(values * values, axis=-1, keepdims=True) + eps)
        * gain.astype(jnp.float32)
    )


def slot_layout(lengths, slot_count):
    ends = jnp.cumsum(lengths)
    starts = ends - lengths
    slot_ids = jnp.arange(slot_count, dtype=jnp.int32)
    request_of = jnp.sum((slot_ids[:, None] >= ends[None, :]).astype(jnp.int32), axis=1)
    picks = (request_of[:, None] == jnp.arange(lengths.shape[0], dtype=jnp.int32)[None, :]).astype(
        jnp.int32
    )
    start_of = jnp.sum(picks * starts[None, :], axis=1)
    positions = PREFIX + slot_ids - start_of
    return (request_of, request_of < lengths.shape[0], positions)


def partial_attention(grouped_queries, key_block, value_block, allowed):
    scores = jnp.einsum(
        "qkgd,nkd->kgqn", grouped_queries, key_block, preferred_element_type=jnp.float32
    ) / math.sqrt(grouped_queries.shape[-1])
    if allowed is not None:
        scores = jnp.where(allowed[None, None], scores, -jnp.inf)
    peak = jnp.max(scores, axis=-1)
    weights = jnp.exp(scores - peak[..., None])
    weight_sum = jnp.sum(weights, axis=-1)
    summed = jnp.einsum(
        "kgqn,nkd->kgqd",
        weights.astype(jnp.bfloat16),
        value_block,
        preferred_element_type=jnp.float32,
    )
    return (summed, peak, weight_sum)


def combine_states(former, latter):
    peak = jnp.maximum(former[1], latter[1])
    scale_former = jnp.exp(former[1] - peak)
    scale_latter = jnp.exp(latter[1] - peak)
    summed = former[0] * scale_former[..., None] + latter[0] * scale_latter[..., None]
    return (summed, peak, former[2] * scale_former + latter[2] * scale_latter)


def layer(
    hidden_in,
    attn_gain,
    w_query,
    w_key,
    w_value,
    w_out,
    mlp_gain,
    w_gate,
    w_up,
    w_down,
    prefix_kv,
    suffix_lengths,
    prefix_owner,
):
    slots_here = hidden_in.shape[0]
    head_dim = HEAD_DIM
    kv_heads = w_key.shape[1] // head_dim
    q_heads = w_query.shape[1] // head_dim
    group = q_heads // kv_heads
    block_len = prefix_kv.shape[0]
    span_bits = GSPAN.bit_length() - 1
    unit_count = w_gate.shape[1]
    n_rx = lax.axis_size("rx")
    n_rc = lax.axis_size("rc")
    n_mlp = lax.axis_size("mlp")
    n_req = n_rx * n_rc
    req_index = lax.axis_index("rx") * n_rc + lax.axis_index("rc")
    mlp_index = lax.axis_index("mlp")

    width_part = w_gate.shape[0]
    gate_up_part = jnp.concatenate([w_gate, w_up], axis=1)
    gate_up_pair = lax.all_gather(gate_up_part, ("rc", "mlp"), axis=0, tiled=False)
    gate_up_pair = gate_up_pair.reshape(n_rc, n_mlp * width_part, 2 * unit_count)
    down_pair = lax.all_gather(w_down, ("rc", "mlp"), axis=0, tiled=False)
    down_pair = down_pair.reshape(n_rc, n_mlp, unit_count, width_part)

    request_of, live, positions = slot_layout(suffix_lengths[0], slots_here)
    hidden_f = hidden_in.astype(jnp.float32)
    normed = rms_norm(hidden_f, attn_gain).astype(jnp.bfloat16)
    query_rows = rope(
        jnp.dot(normed, w_query, preferred_element_type=jnp.float32).reshape(
            slots_here, q_heads, head_dim
        ),
        positions,
    ).astype(jnp.bfloat16)
    key_rows = rope(
        jnp.dot(normed, w_key, preferred_element_type=jnp.float32).reshape(
            slots_here, kv_heads, head_dim
        ),
        positions,
    ).astype(jnp.bfloat16)
    value_rows = (
        jnp.dot(normed, w_value, preferred_element_type=jnp.float32)
        .astype(jnp.bfloat16)
        .reshape(slots_here, kv_heads, head_dim)
    )
    grouped_queries = query_rows.reshape(slots_here, kv_heads, group, head_dim)
    place = req_index % GSPAN
    group_id = req_index // GSPAN
    owners = lax.dynamic_index_in_dim(prefix_owner, group_id, 0, keepdims=False)
    quarter = jnp.sum(jnp.where(owners == place, jnp.arange(GSPAN, dtype=jnp.int32), 0))
    prefix_pos = quarter * block_len + jnp.arange(block_len, dtype=jnp.int32)
    stored_keys = rope(
        prefix_kv[:, 0].reshape(block_len, kv_heads, head_dim).astype(jnp.float32), prefix_pos
    ).astype(jnp.bfloat16)
    stored_values = prefix_kv[:, 1].reshape(block_len, kv_heads, head_dim)
    blocks = jnp.stack([stored_keys, stored_values], axis=0)
    for bit_pos in range(span_bits):
        remote = from_partner(blocks, REQ, bit_pos, n_req)
        blocks = jnp.concatenate([blocks, remote], axis=1)
    prefix_state = partial_attention(grouped_queries, blocks[0], blocks[1], None)
    slot_ids = jnp.arange(slots_here, dtype=jnp.int32)
    allowed = (request_of[:, None] == request_of[None, :]) & (
        slot_ids[None, :] <= slot_ids[:, None]
    )
    suffix_state = partial_attention(grouped_queries, key_rows, value_rows, allowed)
    merged, _, weight_sum = combine_states(prefix_state, suffix_state)
    attended = (
        jnp.transpose(merged / weight_sum[..., None], (2, 0, 1, 3))
        .reshape(slots_here, q_heads * head_dim)
        .astype(jnp.bfloat16)
    )

    head_terms = jnp.dot(attended, w_out, preferred_element_type=jnp.float32)
    head_rows = lax.psum_scatter(head_terms, "mlp", scatter_dimension=0, tiled=True)
    rows_here = slots_here // n_mlp
    row_start = mlp_index * rows_here
    hidden_rows = lax.dynamic_slice_in_dim(hidden_f, row_start, rows_here, 0)
    live_rows = lax.dynamic_slice_in_dim(live, row_start, rows_here, 0)
    residual = (hidden_rows + head_rows).astype(jnp.bfloat16)
    normed_mlp = rms_norm(residual.astype(jnp.float32), mlp_gain).astype(jnp.bfloat16)

    tokens = lax.all_gather(normed_mlp, "rx", axis=0, tiled=True)
    acts = []
    for core in range(n_rc):
        gate_up = jnp.dot(tokens, gate_up_pair[core], preferred_element_type=jnp.float32)
        gate = gate_up[:, :unit_count]
        up_part = gate_up[:, unit_count:]
        acts.append((jax.nn.silu(gate) * up_part).astype(jnp.bfloat16))
    down_sum = None
    for core in range(n_rc):
        term = jnp.einsum(
            "tu,mud->tmd", acts[core], down_pair[core], preferred_element_type=jnp.float32
        ).astype(jnp.bfloat16)
        term = term.reshape(term.shape[0], -1).astype(jnp.float32)
        down_sum = term if down_sum is None else down_sum + term
    down = lax.psum_scatter(
        down_sum.astype(jnp.bfloat16), "rx", scatter_dimension=0, tiled=True
    ).astype(jnp.float32)
    out_rows = jnp.where(
        live_rows[:, None], residual.astype(jnp.float32) + down, 0.0
    ).astype(jnp.bfloat16)
    hidden_out = lax.all_to_all(out_rows, "mlp", 1, 0, tiled=True)

    stacked_kv = jnp.stack(
        [
            key_rows.reshape(slots_here, kv_heads * head_dim),
            value_rows.reshape(slots_here, kv_heads * head_dim),
        ],
        axis=1,
    )
    suffix_kv = jnp.where(live[:, None, None], stacked_kv, jnp.zeros_like(stacked_kv))
    return (hidden_out, suffix_kv)


def solution(mesh):
    req_size, mlp_size = mesh.devices.shape
    view = Mesh(
        np.asarray(mesh.devices).reshape(req_size // 2, 2, mlp_size), ("rx", "rc", "mlp")
    )
    placed = (
        P(REQ, None),
        P(),
        P(None, "mlp"),
        P(None, "mlp"),
        P(None, "mlp"),
        P("mlp", None),
        P(),
        P("mlp", REQ),
        P("mlp", REQ),
        P(REQ, "mlp"),
        P(REQ, None, "mlp"),
        P(REQ, None),
        P(),
    )
    return jax.shard_map(
        layer,
        mesh=view,
        in_specs=placed,
        out_specs=(P(REQ, "mlp"), P(REQ, None, "mlp")),
        check_vma=False,
    )
```

```python
import math

import jax
import jax.numpy as jnp
import numpy as np
from jax import lax
from jax.sharding import Mesh
from jax.sharding import PartitionSpec as P


HEAD_DIM = 128
PREFIX = 8192
GSPAN = 4

REQ = ("ax", "az", "rc")

rope_base = 500000.0
eps = 1e-05


def swap_with_partner(value, axis, size):
    return lax.ppermute(value, axis, [(source, source ^ 1) for source in range(size)])


def rope(values, positions):
    half = values.shape[-1] // 2
    freq = rope_base ** (-jnp.arange(half, dtype=jnp.float32) * 2.0 / values.shape[-1])
    angle = positions.astype(jnp.float32)[:, None] * freq[None, :]
    cosine = jnp.cos(angle)[:, None, :]
    sine = jnp.sin(angle)[:, None, :]
    former = values[..., :half]
    latter = values[..., half:]
    return jnp.concatenate(
        [former * cosine - latter * sine, latter * cosine + former * sine], axis=-1
    )


def rms_norm(values, gain):
    return (
        values
        * lax.rsqrt(jnp.mean(values * values, axis=-1, keepdims=True) + eps)
        * gain.astype(jnp.float32)
    )


def slot_layout(lengths, slot_count):
    ends = jnp.cumsum(lengths)
    starts = ends - lengths
    slot_ids = jnp.arange(slot_count, dtype=jnp.int32)
    request_of = jnp.sum((slot_ids[:, None] >= ends[None, :]).astype(jnp.int32), axis=1)
    picks = (request_of[:, None] == jnp.arange(lengths.shape[0], dtype=jnp.int32)[None, :]).astype(
        jnp.int32
    )
    start_of = jnp.sum(picks * starts[None, :], axis=1)
    positions = PREFIX + slot_ids - start_of
    return (request_of, request_of < lengths.shape[0], positions)


def partial_attention(grouped_queries, key_block, value_block, allowed):
    scores = jnp.einsum(
        "qkgd,nkd->kgqn", grouped_queries, key_block, preferred_element_type=jnp.float32
    ) / math.sqrt(grouped_queries.shape[-1])
    if allowed is not None:
        scores = jnp.where(allowed[None, None], scores, -jnp.inf)
    peak = jnp.max(scores, axis=-1)
    weights = jnp.exp(scores - peak[..., None])
    weight_sum = jnp.sum(weights, axis=-1)
    summed = jnp.einsum(
        "kgqn,nkd->kgqd",
        weights.astype(jnp.bfloat16),
        value_block,
        preferred_element_type=jnp.float32,
    )
    return jnp.concatenate([summed, peak[..., None], weight_sum[..., None]], axis=-1)


def combine_states(former, latter):
    head_dim = former.shape[-1] - 2
    peak = jnp.maximum(former[..., head_dim], latter[..., head_dim])
    scale_former = jnp.exp(former[..., head_dim] - peak)
    scale_latter = jnp.exp(latter[..., head_dim] - peak)
    summed = (
        former[..., :head_dim] * scale_former[..., None]
        + latter[..., :head_dim] * scale_latter[..., None]
    )
    weight_sum = (
        former[..., head_dim + 1] * scale_former + latter[..., head_dim + 1] * scale_latter
    )
    return jnp.concatenate([summed, peak[..., None], weight_sum[..., None]], axis=-1)


def layer(
    hidden_in,
    attn_gain,
    w_query,
    w_key,
    w_value,
    w_out,
    mlp_gain,
    w_gate,
    w_up,
    w_down,
    prefix_kv,
    suffix_lengths,
    prefix_owner,
):
    slots_here = hidden_in.shape[0]
    head_dim = HEAD_DIM
    kv_heads = w_key.shape[1] // head_dim
    q_heads = w_query.shape[1] // head_dim
    group = q_heads // kv_heads
    block_len = prefix_kv.shape[0]
    unit_count = w_gate.shape[1]
    width_part = w_gate.shape[0]
    n_az = lax.axis_size("az")
    n_rc = lax.axis_size("rc")
    n_mlp = lax.axis_size("mlp")
    az_index = lax.axis_index("az")
    rc_index = lax.axis_index("rc")
    req_index = (lax.axis_index("ax") * n_az + az_index) * n_rc + rc_index
    mlp_index = lax.axis_index("mlp")

    gate_up_part = jnp.concatenate([w_gate, w_up], axis=1)
    gate_up_pair = lax.all_gather(gate_up_part, ("rc", "mlp"), axis=0, tiled=False)
    gate_up_pair = gate_up_pair.reshape(n_rc, n_mlp * width_part, 2 * unit_count)
    down_pair = lax.all_gather(w_down, ("rc", "mlp"), axis=0, tiled=False)
    down_pair = down_pair.reshape(n_rc, n_mlp, unit_count, width_part)

    request_of, live, positions = slot_layout(suffix_lengths[0], slots_here)
    hidden_f = hidden_in.astype(jnp.float32)
    normed = rms_norm(hidden_f, attn_gain).astype(jnp.bfloat16)
    query_rows = rope(
        jnp.dot(normed, w_query, preferred_element_type=jnp.float32).reshape(
            slots_here, q_heads, head_dim
        ),
        positions,
    ).astype(jnp.bfloat16)
    key_rows = rope(
        jnp.dot(normed, w_key, preferred_element_type=jnp.float32).reshape(
            slots_here, kv_heads, head_dim
        ),
        positions,
    ).astype(jnp.bfloat16)
    value_rows = (
        jnp.dot(normed, w_value, preferred_element_type=jnp.float32)
        .astype(jnp.bfloat16)
        .reshape(slots_here, kv_heads, head_dim)
    )
    grouped_queries = query_rows.reshape(slots_here, kv_heads, group, head_dim)

    place = req_index % GSPAN
    group_id = req_index // GSPAN
    owners = lax.dynamic_index_in_dim(prefix_owner, group_id, 0, keepdims=False)
    quarter = jnp.sum(jnp.where(owners == place, jnp.arange(GSPAN, dtype=jnp.int32), 0))
    prefix_pos = quarter * block_len + jnp.arange(block_len, dtype=jnp.int32)
    stored_keys = rope(
        prefix_kv[:, 0].reshape(block_len, kv_heads, head_dim).astype(jnp.float32), prefix_pos
    ).astype(jnp.bfloat16)
    stored_values = prefix_kv[:, 1].reshape(block_len, kv_heads, head_dim)

    z_bit = az_index % 2
    core_other = swap_with_partner(grouped_queries, "rc", n_rc)
    pair = jnp.where(
        rc_index == 0,
        jnp.stack([grouped_queries, core_other]),
        jnp.stack([core_other, grouped_queries]),
    )
    z_other = swap_with_partner(pair, "az", n_az)
    group_queries = jnp.where(
        z_bit == 0, jnp.concatenate([pair, z_other]), jnp.concatenate([z_other, pair])
    )
    runs = group_queries.shape[0]
    states = partial_attention(
        group_queries.reshape(runs * slots_here, kv_heads, group, head_dim),
        stored_keys,
        stored_values,
        None,
    )
    states = states.reshape(kv_heads, group, runs, slots_here, head_dim + 2)
    keep = lax.dynamic_slice_in_dim(states, z_bit * 2, 2, 2)
    send = lax.dynamic_slice_in_dim(states, (1 - z_bit) * 2, 2, 2)
    states = combine_states(keep, swap_with_partner(send, "az", n_az))
    keep = lax.dynamic_slice_in_dim(states, rc_index, 1, 2)
    send = lax.dynamic_slice_in_dim(states, 1 - rc_index, 1, 2)
    prefix_state = combine_states(keep, swap_with_partner(send, "rc", n_rc))[:, :, 0]

    slot_ids = jnp.arange(slots_here, dtype=jnp.int32)
    allowed = (request_of[:, None] == request_of[None, :]) & (
        slot_ids[None, :] <= slot_ids[:, None]
    )
    suffix_state = partial_attention(grouped_queries, key_rows, value_rows, allowed)
    merged = combine_states(prefix_state, suffix_state)
    attended = (
        jnp.transpose(merged[..., :head_dim] / merged[..., head_dim + 1 :], (2, 0, 1, 3))
        .reshape(slots_here, q_heads * head_dim)
        .astype(jnp.bfloat16)
    )

    head_terms = jnp.dot(attended, w_out, preferred_element_type=jnp.float32)
    head_rows = lax.psum_scatter(head_terms, "mlp", scatter_dimension=0, tiled=True)
    rows_here = slots_here // n_mlp
    row_start = mlp_index * rows_here
    hidden_rows = lax.dynamic_slice_in_dim(hidden_f, row_start, rows_here, 0)
    live_rows = lax.dynamic_slice_in_dim(live, row_start, rows_here, 0)
    residual = (hidden_rows + head_rows).astype(jnp.bfloat16)
    normed_mlp = rms_norm(residual.astype(jnp.float32), mlp_gain).astype(jnp.bfloat16)

    tokens = lax.all_gather(normed_mlp, "az", axis=0, tiled=True)
    tokens = lax.all_gather(tokens, "ax", axis=0, tiled=True)
    acts = []
    for core in range(n_rc):
        gate_up = jnp.dot(tokens, gate_up_pair[core], preferred_element_type=jnp.float32)
        gate = gate_up[:, :unit_count]
        up_part = gate_up[:, unit_count:]
        acts.append((jax.nn.silu(gate) * up_part).astype(jnp.bfloat16))
    down_sum = None
    for core in range(n_rc):
        term = jnp.einsum(
            "tu,mud->tmd", acts[core], down_pair[core], preferred_element_type=jnp.float32
        ).astype(jnp.bfloat16)
        term = term.reshape(term.shape[0], -1).astype(jnp.float32)
        down_sum = term if down_sum is None else down_sum + term
    down = lax.psum_scatter(down_sum.astype(jnp.bfloat16), "ax", scatter_dimension=0, tiled=True)
    down = lax.psum_scatter(down, "az", scatter_dimension=0, tiled=True).astype(jnp.float32)
    out_rows = jnp.where(
        live_rows[:, None], residual.astype(jnp.float32) + down, 0.0
    ).astype(jnp.bfloat16)
    hidden_out = lax.all_to_all(out_rows, "mlp", 1, 0, tiled=True)

    stacked_kv = jnp.stack(
        [
            key_rows.reshape(slots_here, kv_heads * head_dim),
            value_rows.reshape(slots_here, kv_heads * head_dim),
        ],
        axis=1,
    )
    suffix_kv = jnp.where(live[:, None, None], stacked_kv, jnp.zeros_like(stacked_kv))
    return (hidden_out, suffix_kv)


def solution(mesh):
    req_size, mlp_size = mesh.devices.shape
    x_size = req_size // 8
    view = Mesh(
        np.asarray(mesh.devices).reshape(x_size, 4, 2, mlp_size), ("ax", "az", "rc", "mlp")
    )
    placed = (
        P(REQ, None),
        P(),
        P(None, "mlp"),
        P(None, "mlp"),
        P(None, "mlp"),
        P("mlp", None),
        P(),
        P("mlp", REQ),
        P("mlp", REQ),
        P(REQ, "mlp"),
        P(REQ, None, "mlp"),
        P(REQ, None),
        P(),
    )
    return jax.shard_map(
        layer,
        mesh=view,
        in_specs=placed,
        out_specs=(P(REQ, "mlp"), P(REQ, None, "mlp")),
        check_vma=False,
    )
```

```python
import math

import jax
import jax.numpy as jnp
import numpy as np
from jax import lax
from jax.sharding import Mesh
from jax.sharding import PartitionSpec as P


HEAD_DIM = 128
PREFIX = 8192
GSPAN = 4

REQ = ("ax", "az", "rc")

rope_base = 500000.0
eps = 1e-05


def swap_with_partner(value, axis, size):
    return lax.ppermute(value, axis, [(source, source ^ 1) for source in range(size)])


def rope(values, positions):
    half = values.shape[-1] // 2
    freq = rope_base ** (-jnp.arange(half, dtype=jnp.float32) * 2.0 / values.shape[-1])
    angle = positions.astype(jnp.float32)[:, None] * freq[None, :]
    cosine = jnp.cos(angle)[:, None, :]
    sine = jnp.sin(angle)[:, None, :]
    former = values[..., :half]
    latter = values[..., half:]
    return jnp.concatenate(
        [former * cosine - latter * sine, latter * cosine + former * sine], axis=-1
    )


def rms_norm(values, gain):
    return (
        values
        * lax.rsqrt(jnp.mean(values * values, axis=-1, keepdims=True) + eps)
        * gain.astype(jnp.float32)
    )


def slot_layout(lengths, slot_count):
    ends = jnp.cumsum(lengths)
    starts = ends - lengths
    slot_ids = jnp.arange(slot_count, dtype=jnp.int32)
    request_of = jnp.sum((slot_ids[:, None] >= ends[None, :]).astype(jnp.int32), axis=1)
    picks = (request_of[:, None] == jnp.arange(lengths.shape[0], dtype=jnp.int32)[None, :]).astype(
        jnp.int32
    )
    start_of = jnp.sum(picks * starts[None, :], axis=1)
    positions = PREFIX + slot_ids - start_of
    return (request_of, request_of < lengths.shape[0], positions)


def partial_attention(grouped_queries, key_block, value_block, allowed):
    scores = jnp.einsum(
        "qkgd,nkd->kgqn", grouped_queries, key_block, preferred_element_type=jnp.float32
    ) / math.sqrt(grouped_queries.shape[-1])
    if allowed is not None:
        scores = jnp.where(allowed[None, None], scores, -jnp.inf)
    peak = jnp.max(scores, axis=-1)
    weights = jnp.exp(scores - peak[..., None])
    weight_sum = jnp.sum(weights, axis=-1)
    summed = jnp.einsum(
        "kgqn,nkd->kgqd",
        weights.astype(jnp.bfloat16),
        value_block,
        preferred_element_type=jnp.float32,
    )
    return jnp.concatenate([summed, peak[..., None], weight_sum[..., None]], axis=-1)


def combine_states(former, latter):
    head_dim = former.shape[-1] - 2
    peak = jnp.maximum(former[..., head_dim], latter[..., head_dim])
    scale_former = jnp.exp(former[..., head_dim] - peak)
    scale_latter = jnp.exp(latter[..., head_dim] - peak)
    summed = (
        former[..., :head_dim] * scale_former[..., None]
        + latter[..., :head_dim] * scale_latter[..., None]
    )
    weight_sum = (
        former[..., head_dim + 1] * scale_former + latter[..., head_dim + 1] * scale_latter
    )
    return jnp.concatenate([summed, peak[..., None], weight_sum[..., None]], axis=-1)


def layer(
    hidden_in,
    attn_gain,
    w_query,
    w_key,
    w_value,
    w_out,
    mlp_gain,
    w_gate,
    w_up,
    w_down,
    prefix_kv,
    suffix_lengths,
    prefix_owner,
):
    slots_here = hidden_in.shape[0]
    head_dim = HEAD_DIM
    kv_heads = w_key.shape[1] // head_dim
    q_heads = w_query.shape[1] // head_dim
    group = q_heads // kv_heads
    block_len = prefix_kv.shape[0]
    unit_count = w_gate.shape[1]
    width_part = w_gate.shape[0]
    n_az = lax.axis_size("az")
    n_rc = lax.axis_size("rc")
    n_mlp = lax.axis_size("mlp")
    az_index = lax.axis_index("az")
    rc_index = lax.axis_index("rc")
    req_index = (lax.axis_index("ax") * n_az + az_index) * n_rc + rc_index
    mlp_index = lax.axis_index("mlp")

    own = (jnp.concatenate([w_gate, w_up], axis=1), w_down)
    from_left = lax.ppermute(own, "mlp", [(i, (i + 1) % n_mlp) for i in range(n_mlp)])
    from_right = lax.ppermute(own, "mlp", [(i, (i - 1) % n_mlp) for i in range(n_mlp)])
    half_gu = width_part // 2
    half_wd = unit_count // 2
    relay_a = lax.ppermute(
        (from_left[0][:half_gu], from_left[1][:half_wd]),
        "mlp",
        [(i, (i + 1) % n_mlp) for i in range(n_mlp)],
    )
    relay_b = lax.ppermute(
        (from_right[0][half_gu:], from_right[1][half_wd:]),
        "mlp",
        [(i, (i - 1) % n_mlp) for i in range(n_mlp)],
    )
    across = (
        jnp.concatenate([relay_a[0], relay_b[0]], axis=0),
        jnp.concatenate([relay_a[1], relay_b[1]], axis=0),
    )
    gate_up_ring = jnp.stack([own[0], from_left[0], across[0], from_right[0]])
    down_ring = jnp.stack([own[1], from_left[1], across[1], from_right[1]])
    gate_up_other, down_other = swap_with_partner((gate_up_ring, down_ring), "rc", n_rc)
    gate_up_pair = (gate_up_ring, gate_up_other)
    down_pair = (down_ring, down_other)
    quarter_of = [(mlp_index - ring) % n_mlp for ring in range(n_mlp)]

    request_of, live, positions = slot_layout(suffix_lengths[0], slots_here)
    hidden_f = hidden_in.astype(jnp.float32)
    normed = rms_norm(hidden_f, attn_gain).astype(jnp.bfloat16)
    query_rows = rope(
        jnp.dot(normed, w_query, preferred_element_type=jnp.float32).reshape(
            slots_here, q_heads, head_dim
        ),
        positions,
    ).astype(jnp.bfloat16)
    key_rows = rope(
        jnp.dot(normed, w_key, preferred_element_type=jnp.float32).reshape(
            slots_here, kv_heads, head_dim
        ),
        positions,
    ).astype(jnp.bfloat16)
    value_rows = (
        jnp.dot(normed, w_value, preferred_element_type=jnp.float32)
        .astype(jnp.bfloat16)
        .reshape(slots_here, kv_heads, head_dim)
    )
    grouped_queries = query_rows.reshape(slots_here, kv_heads, group, head_dim)

    place = req_index % GSPAN
    group_id = req_index // GSPAN
    owners = lax.dynamic_index_in_dim(prefix_owner, group_id, 0, keepdims=False)
    quarter = jnp.sum(jnp.where(owners == place, jnp.arange(GSPAN, dtype=jnp.int32), 0))
    prefix_pos = quarter * block_len + jnp.arange(block_len, dtype=jnp.int32)
    stored_keys = rope(
        prefix_kv[:, 0].reshape(block_len, kv_heads, head_dim).astype(jnp.float32), prefix_pos
    ).astype(jnp.bfloat16)
    stored_values = prefix_kv[:, 1].reshape(block_len, kv_heads, head_dim)

    z_bit = az_index % 2
    core_other = swap_with_partner(grouped_queries, "rc", n_rc)
    pair = jnp.where(
        rc_index == 0,
        jnp.stack([grouped_queries, core_other]),
        jnp.stack([core_other, grouped_queries]),
    )
    z_other = swap_with_partner(pair, "az", n_az)
    group_queries = jnp.where(
        z_bit == 0, jnp.concatenate([pair, z_other]), jnp.concatenate([z_other, pair])
    )
    runs = group_queries.shape[0]
    states = partial_attention(
        group_queries.reshape(runs * slots_here, kv_heads, group, head_dim),
        stored_keys,
        stored_values,
        None,
    )
    states = states.reshape(kv_heads, group, runs, slots_here, head_dim + 2)
    keep = lax.dynamic_slice_in_dim(states, z_bit * 2, 2, 2)
    send = lax.dynamic_slice_in_dim(states, (1 - z_bit) * 2, 2, 2)
    states = combine_states(keep, swap_with_partner(send, "az", n_az))
    keep = lax.dynamic_slice_in_dim(states, rc_index, 1, 2)
    send = lax.dynamic_slice_in_dim(states, 1 - rc_index, 1, 2)
    prefix_state = combine_states(keep, swap_with_partner(send, "rc", n_rc))[:, :, 0]

    slot_ids = jnp.arange(slots_here, dtype=jnp.int32)
    allowed = (request_of[:, None] == request_of[None, :]) & (
        slot_ids[None, :] <= slot_ids[:, None]
    )
    suffix_state = partial_attention(grouped_queries, key_rows, value_rows, allowed)
    merged = combine_states(prefix_state, suffix_state)
    attended = (
        jnp.transpose(merged[..., :head_dim] / merged[..., head_dim + 1 :], (2, 0, 1, 3))
        .reshape(slots_here, q_heads * head_dim)
        .astype(jnp.bfloat16)
    )

    head_terms = jnp.dot(attended, w_out, preferred_element_type=jnp.float32)
    head_rows = lax.psum_scatter(head_terms, "mlp", scatter_dimension=0, tiled=True)
    rows_here = slots_here // n_mlp
    row_start = mlp_index * rows_here
    hidden_rows = lax.dynamic_slice_in_dim(hidden_f, row_start, rows_here, 0)
    live_rows = lax.dynamic_slice_in_dim(live, row_start, rows_here, 0)
    residual = (hidden_rows + head_rows).astype(jnp.bfloat16)
    normed_mlp = rms_norm(residual.astype(jnp.float32), mlp_gain).astype(jnp.bfloat16)

    tokens = lax.all_gather(normed_mlp, REQ[:2], axis=0, tiled=True)
    tokens_ring = jnp.concatenate(
        [
            lax.dynamic_slice_in_dim(tokens, quarter_of[ring] * width_part, width_part, 1)
            for ring in range(n_mlp)
        ],
        axis=1,
    )
    acts = []
    for core in range(n_rc):
        weights_here = gate_up_pair[core].reshape(n_mlp * width_part, 2 * unit_count)
        gate_up = jnp.dot(tokens_ring, weights_here, preferred_element_type=jnp.float32)
        gate = gate_up[:, :unit_count]
        up_part = gate_up[:, unit_count:]
        acts.append((jax.nn.silu(gate) * up_part).astype(jnp.bfloat16))
    down_sum = None
    for core in range(n_rc):
        term = jnp.einsum(
            "tu,mud->tmd", acts[core], down_pair[core], preferred_element_type=jnp.float32
        ).astype(jnp.bfloat16)
        term = term.reshape(term.shape[0], -1).astype(jnp.float32)
        down_sum = term if down_sum is None else down_sum + term
    down = lax.psum_scatter(down_sum.astype(jnp.bfloat16), "ax", scatter_dimension=0, tiled=True)
    down = lax.psum_scatter(down, "az", scatter_dimension=0, tiled=True)
    down = down.reshape(rows_here, n_mlp, width_part)
    natural = jnp.stack([(mlp_index - j) % n_mlp for j in range(n_mlp)])
    down = jnp.take(down, natural, axis=1).reshape(rows_here, n_mlp * width_part)
    down = down.astype(jnp.float32)
    out_rows = jnp.where(
        live_rows[:, None], residual.astype(jnp.float32) + down, 0.0
    ).astype(jnp.bfloat16)
    hidden_out = lax.all_to_all(out_rows, "mlp", 1, 0, tiled=True)

    stacked_kv = jnp.stack(
        [
            key_rows.reshape(slots_here, kv_heads * head_dim),
            value_rows.reshape(slots_here, kv_heads * head_dim),
        ],
        axis=1,
    )
    suffix_kv = jnp.where(live[:, None, None], stacked_kv, jnp.zeros_like(stacked_kv))
    return (hidden_out, suffix_kv)


def solution(mesh):
    req_size, mlp_size = mesh.devices.shape
    x_size = req_size // 8
    view = Mesh(
        np.asarray(mesh.devices).reshape(x_size, 4, 2, mlp_size), ("ax", "az", "rc", "mlp")
    )
    placed = (
        P(REQ, None),
        P(),
        P(None, "mlp"),
        P(None, "mlp"),
        P(None, "mlp"),
        P("mlp", None),
        P(),
        P("mlp", REQ),
        P("mlp", REQ),
        P(REQ, "mlp"),
        P(REQ, None, "mlp"),
        P(REQ, None),
        P(),
    )
    return jax.shard_map(
        layer,
        mesh=view,
        in_specs=placed,
        out_specs=(P(REQ, "mlp"), P(REQ, None, "mlp")),
        check_vma=False,
    )
```

```python
import math

import jax
import jax.numpy as jnp
import numpy as np
from jax import lax
from jax.sharding import Mesh
from jax.sharding import PartitionSpec as P


HEAD_DIM = 128
PREFIX = 8192
GSPAN = 4

REQ = ("ax", "az", "rc")

rope_base = 500000.0
eps = 1e-05


def swap_with_partner(value, axis, size):
    return lax.ppermute(value, axis, [(source, source ^ 1) for source in range(size)])


def rope(values, positions):
    half = values.shape[-1] // 2
    freq = rope_base ** (-jnp.arange(half, dtype=jnp.float32) * 2.0 / values.shape[-1])
    angle = positions.astype(jnp.float32)[:, None] * freq[None, :]
    cosine = jnp.cos(angle)[:, None, :]
    sine = jnp.sin(angle)[:, None, :]
    former = values[..., :half]
    latter = values[..., half:]
    return jnp.concatenate(
        [former * cosine - latter * sine, latter * cosine + former * sine], axis=-1
    )


def rms_norm(values, gain):
    return (
        values
        * lax.rsqrt(jnp.mean(values * values, axis=-1, keepdims=True) + eps)
        * gain.astype(jnp.float32)
    )


def slot_layout(lengths, slot_count):
    ends = jnp.cumsum(lengths)
    starts = ends - lengths
    slot_ids = jnp.arange(slot_count, dtype=jnp.int32)
    request_of = jnp.sum((slot_ids[:, None] >= ends[None, :]).astype(jnp.int32), axis=1)
    picks = (request_of[:, None] == jnp.arange(lengths.shape[0], dtype=jnp.int32)[None, :]).astype(
        jnp.int32
    )
    start_of = jnp.sum(picks * starts[None, :], axis=1)
    positions = PREFIX + slot_ids - start_of
    return (request_of, request_of < lengths.shape[0], positions)


def partial_attention(grouped_queries, key_block, value_block, allowed):
    scores = jnp.einsum(
        "qkgd,nkd->kgqn", grouped_queries, key_block, preferred_element_type=jnp.float32
    ) / math.sqrt(grouped_queries.shape[-1])
    if allowed is not None:
        scores = jnp.where(allowed[None, None], scores, -jnp.inf)
    peak = jnp.max(scores, axis=-1)
    weights = jnp.exp(scores - peak[..., None])
    weight_sum = jnp.sum(weights, axis=-1)
    summed = jnp.einsum(
        "kgqn,nkd->kgqd",
        weights.astype(jnp.bfloat16),
        value_block,
        preferred_element_type=jnp.float32,
    )
    return jnp.concatenate([summed, peak[..., None], weight_sum[..., None]], axis=-1)


def combine_states(former, latter):
    head_dim = former.shape[-1] - 2
    peak = jnp.maximum(former[..., head_dim], latter[..., head_dim])
    scale_former = jnp.exp(former[..., head_dim] - peak)
    scale_latter = jnp.exp(latter[..., head_dim] - peak)
    summed = (
        former[..., :head_dim] * scale_former[..., None]
        + latter[..., :head_dim] * scale_latter[..., None]
    )
    weight_sum = (
        former[..., head_dim + 1] * scale_former + latter[..., head_dim + 1] * scale_latter
    )
    return jnp.concatenate([summed, peak[..., None], weight_sum[..., None]], axis=-1)


def layer(
    hidden_in,
    attn_gain,
    w_query,
    w_key,
    w_value,
    w_out,
    mlp_gain,
    w_gate,
    w_up,
    w_down,
    prefix_kv,
    suffix_lengths,
    prefix_owner,
):
    slots_here = hidden_in.shape[0]
    head_dim = HEAD_DIM
    kv_heads = w_key.shape[1] // head_dim
    q_heads = w_query.shape[1] // head_dim
    group = q_heads // kv_heads
    block_len = prefix_kv.shape[0]
    unit_count = w_gate.shape[1]
    width_part = w_gate.shape[0]
    n_az = lax.axis_size("az")
    n_rc = lax.axis_size("rc")
    n_mlp = lax.axis_size("mlp")
    az_index = lax.axis_index("az")
    rc_index = lax.axis_index("rc")
    req_index = (lax.axis_index("ax") * n_az + az_index) * n_rc + rc_index
    mlp_index = lax.axis_index("mlp")

    own = (jnp.concatenate([w_gate, w_up], axis=1), w_down)
    from_left = lax.ppermute(own, "mlp", [(i, (i + 1) % n_mlp) for i in range(n_mlp)])
    from_right = lax.ppermute(own, "mlp", [(i, (i - 1) % n_mlp) for i in range(n_mlp)])
    half_gu = width_part // 2
    half_wd = unit_count // 2
    relay_a = lax.ppermute(
        (from_left[0][:half_gu], from_left[1][:half_wd]),
        "mlp",
        [(i, (i + 1) % n_mlp) for i in range(n_mlp)],
    )
    relay_b = lax.ppermute(
        (from_right[0][half_gu:], from_right[1][half_wd:]),
        "mlp",
        [(i, (i - 1) % n_mlp) for i in range(n_mlp)],
    )
    across = (
        jnp.concatenate([relay_a[0], relay_b[0]], axis=0),
        jnp.concatenate([relay_a[1], relay_b[1]], axis=0),
    )
    gate_up_ring = jnp.stack([own[0], from_left[0], across[0], from_right[0]])
    down_ring = jnp.stack([own[1], from_left[1], across[1], from_right[1]], axis=1)
    down_ring = down_ring.reshape(unit_count, n_mlp * width_part)
    gate_up_other, down_other = swap_with_partner((gate_up_ring, down_ring), "rc", n_rc)
    gate_up_pair = (gate_up_ring, gate_up_other)
    down_pair = (down_ring, down_other)
    quarter_of = [(mlp_index - ring) % n_mlp for ring in range(n_mlp)]

    request_of, live, positions = slot_layout(suffix_lengths[0], slots_here)
    hidden_f = hidden_in.astype(jnp.float32)
    normed = rms_norm(hidden_f, attn_gain).astype(jnp.bfloat16)
    query_rows = rope(
        jnp.dot(normed, w_query, preferred_element_type=jnp.float32).reshape(
            slots_here, q_heads, head_dim
        ),
        positions,
    ).astype(jnp.bfloat16)
    key_rows = rope(
        jnp.dot(normed, w_key, preferred_element_type=jnp.float32).reshape(
            slots_here, kv_heads, head_dim
        ),
        positions,
    ).astype(jnp.bfloat16)
    value_rows = (
        jnp.dot(normed, w_value, preferred_element_type=jnp.float32)
        .astype(jnp.bfloat16)
        .reshape(slots_here, kv_heads, head_dim)
    )
    grouped_queries = query_rows.reshape(slots_here, kv_heads, group, head_dim)

    place = req_index % GSPAN
    group_id = req_index // GSPAN
    owners = lax.dynamic_index_in_dim(prefix_owner, group_id, 0, keepdims=False)
    quarter = jnp.sum(jnp.where(owners == place, jnp.arange(GSPAN, dtype=jnp.int32), 0))
    prefix_pos = quarter * block_len + jnp.arange(block_len, dtype=jnp.int32)
    stored_keys = rope(
        prefix_kv[:, 0].reshape(block_len, kv_heads, head_dim).astype(jnp.float32), prefix_pos
    ).astype(jnp.bfloat16)
    stored_values = prefix_kv[:, 1].reshape(block_len, kv_heads, head_dim)

    z_bit = az_index % 2
    core_other = swap_with_partner(grouped_queries, "rc", n_rc)
    pair = jnp.where(
        rc_index == 0,
        jnp.stack([grouped_queries, core_other]),
        jnp.stack([core_other, grouped_queries]),
    )
    z_other = swap_with_partner(pair, "az", n_az)
    group_queries = jnp.where(
        z_bit == 0, jnp.concatenate([pair, z_other]), jnp.concatenate([z_other, pair])
    )
    runs = group_queries.shape[0]
    states = partial_attention(
        group_queries.reshape(runs * slots_here, kv_heads, group, head_dim),
        stored_keys,
        stored_values,
        None,
    )
    states = states.reshape(kv_heads, group, runs, slots_here, head_dim + 2)
    keep = lax.dynamic_slice_in_dim(states, z_bit * 2, 2, 2)
    send = lax.dynamic_slice_in_dim(states, (1 - z_bit) * 2, 2, 2)
    states = combine_states(keep, swap_with_partner(send, "az", n_az))
    keep = lax.dynamic_slice_in_dim(states, rc_index, 1, 2)
    send = lax.dynamic_slice_in_dim(states, 1 - rc_index, 1, 2)
    prefix_state = combine_states(keep, swap_with_partner(send, "rc", n_rc))[:, :, 0]

    slot_ids = jnp.arange(slots_here, dtype=jnp.int32)
    allowed = (request_of[:, None] == request_of[None, :]) & (
        slot_ids[None, :] <= slot_ids[:, None]
    )
    suffix_state = partial_attention(grouped_queries, key_rows, value_rows, allowed)
    merged = combine_states(prefix_state, suffix_state)
    attended = (
        jnp.transpose(merged[..., :head_dim] / merged[..., head_dim + 1 :], (2, 0, 1, 3))
        .reshape(slots_here, q_heads * head_dim)
        .astype(jnp.bfloat16)
    )

    head_terms = jnp.dot(attended, w_out, preferred_element_type=jnp.float32)
    head_rows = lax.psum_scatter(head_terms, "mlp", scatter_dimension=0, tiled=True)
    rows_here = slots_here // n_mlp
    row_start = mlp_index * rows_here
    hidden_rows = lax.dynamic_slice_in_dim(hidden_f, row_start, rows_here, 0)
    live_rows = lax.dynamic_slice_in_dim(live, row_start, rows_here, 0)
    residual = (hidden_rows + head_rows).astype(jnp.bfloat16)
    normed_mlp = rms_norm(residual.astype(jnp.float32), mlp_gain).astype(jnp.bfloat16)

    tokens = lax.all_gather(normed_mlp, REQ[:2], axis=0, tiled=True)
    tokens_ring = jnp.concatenate(
        [
            lax.dynamic_slice_in_dim(tokens, quarter_of[ring] * width_part, width_part, 1)
            for ring in range(n_mlp)
        ],
        axis=1,
    )
    acts = []
    for core in range(n_rc):
        weights_here = gate_up_pair[core].reshape(n_mlp * width_part, 2 * unit_count)
        gate_up = jnp.dot(tokens_ring, weights_here, preferred_element_type=jnp.float32)
        gate = gate_up[:, :unit_count]
        up_part = gate_up[:, unit_count:]
        acts.append((jax.nn.silu(gate) * up_part).astype(jnp.bfloat16))
    down_sum = None
    for core in range(n_rc):
        term = jnp.dot(acts[core], down_pair[core], preferred_element_type=jnp.float32)
        term = term.astype(jnp.bfloat16).astype(jnp.float32)
        down_sum = term if down_sum is None else down_sum + term
    down = lax.psum_scatter(down_sum.astype(jnp.bfloat16), "ax", scatter_dimension=0, tiled=True)
    down = lax.psum_scatter(down, "az", scatter_dimension=0, tiled=True)
    down = down.reshape(rows_here, n_mlp, width_part)
    natural = jnp.stack([(mlp_index - j) % n_mlp for j in range(n_mlp)])
    down = jnp.take(down, natural, axis=1).reshape(rows_here, n_mlp * width_part)
    down = down.astype(jnp.float32)
    out_rows = jnp.where(
        live_rows[:, None], residual.astype(jnp.float32) + down, 0.0
    ).astype(jnp.bfloat16)
    hidden_out = lax.all_to_all(out_rows, "mlp", 1, 0, tiled=True)

    stacked_kv = jnp.stack(
        [
            key_rows.reshape(slots_here, kv_heads * head_dim),
            value_rows.reshape(slots_here, kv_heads * head_dim),
        ],
        axis=1,
    )
    suffix_kv = jnp.where(live[:, None, None], stacked_kv, jnp.zeros_like(stacked_kv))
    return (hidden_out, suffix_kv)


def solution(mesh):
    req_size, mlp_size = mesh.devices.shape
    x_size = req_size // 8
    view = Mesh(
        np.asarray(mesh.devices).reshape(x_size, 4, 2, mlp_size), ("ax", "az", "rc", "mlp")
    )
    placed = (
        P(REQ, None),
        P(),
        P(None, "mlp"),
        P(None, "mlp"),
        P(None, "mlp"),
        P("mlp", None),
        P(),
        P("mlp", REQ),
        P("mlp", REQ),
        P(REQ, "mlp"),
        P(REQ, None, "mlp"),
        P(REQ, None),
        P(),
    )
    return jax.shard_map(
        layer,
        mesh=view,
        in_specs=placed,
        out_specs=(P(REQ, "mlp"), P(REQ, None, "mlp")),
        check_vma=False,
    )
```

```python
import math

import jax
import jax.numpy as jnp
import numpy as np
from jax import lax
from jax.sharding import Mesh
from jax.sharding import PartitionSpec as P


HEAD_DIM = 128
PREFIX = 8192
GSPAN = 4

REQ = ("ax", "az", "rc")

rope_base = 500000.0
eps = 1e-05


def shifted(value, axis, size, shift):
    return lax.ppermute(value, axis, [(i, (i + shift) % size) for i in range(size)])


def gather_plane(rows, n_ax, n_az):
    half = rows.shape[1] // 2
    part_a = rows[:, :half]
    part_b = rows[:, half:]
    a_z = jnp.stack([part_a] + [shifted(part_a, "az", n_az, d) for d in range(1, n_az)])
    b_x = jnp.stack([part_b] + [shifted(part_b, "ax", n_ax, d) for d in range(1, n_ax)])
    a_zx = jnp.stack([a_z] + [shifted(a_z, "ax", n_ax, d) for d in range(1, n_ax)])
    b_xz = jnp.stack([b_x] + [shifted(b_x, "az", n_az, d) for d in range(1, n_az)])
    return jnp.concatenate(
        [a_zx.reshape(-1, half), jnp.swapaxes(b_xz, 0, 1).reshape(-1, half)], axis=1
    )


def reduce_plane(blocks, n_ax, n_az):
    rows = blocks.shape[0] // (n_ax * n_az)
    half = blocks.shape[1] // 2
    blocks = blocks.reshape(n_ax, n_az, rows, 2 * half)
    part_a = blocks[..., :half]
    part_b = blocks[..., half:]

    def fold(stack, axis, size):
        total = stack[0].astype(jnp.float32)
        for d in range(1, size):
            total = total + shifted(stack[d], axis, size, -d).astype(jnp.float32)
        return total

    a_1 = fold(part_a, "ax", n_ax).astype(jnp.bfloat16)
    a_2 = fold(a_1, "az", n_az)
    b_1 = fold(jnp.swapaxes(part_b, 0, 1), "az", n_az).astype(jnp.bfloat16)
    b_2 = fold(b_1, "ax", n_ax)
    return jnp.concatenate([a_2, b_2], axis=1)


def swap_with_partner(value, axis, size):
    return lax.ppermute(value, axis, [(source, source ^ 1) for source in range(size)])


def rope(values, positions):
    half = values.shape[-1] // 2
    freq = rope_base ** (-jnp.arange(half, dtype=jnp.float32) * 2.0 / values.shape[-1])
    angle = positions.astype(jnp.float32)[:, None] * freq[None, :]
    cosine = jnp.cos(angle)[:, None, :]
    sine = jnp.sin(angle)[:, None, :]
    former = values[..., :half]
    latter = values[..., half:]
    return jnp.concatenate(
        [former * cosine - latter * sine, latter * cosine + former * sine], axis=-1
    )


def rms_norm(values, gain):
    return (
        values
        * lax.rsqrt(jnp.mean(values * values, axis=-1, keepdims=True) + eps)
        * gain.astype(jnp.float32)
    )


def slot_layout(lengths, slot_count):
    ends = jnp.cumsum(lengths)
    starts = ends - lengths
    slot_ids = jnp.arange(slot_count, dtype=jnp.int32)
    request_of = jnp.sum((slot_ids[:, None] >= ends[None, :]).astype(jnp.int32), axis=1)
    picks = (request_of[:, None] == jnp.arange(lengths.shape[0], dtype=jnp.int32)[None, :]).astype(
        jnp.int32
    )
    start_of = jnp.sum(picks * starts[None, :], axis=1)
    positions = PREFIX + slot_ids - start_of
    return (request_of, request_of < lengths.shape[0], positions)


def partial_attention(grouped_queries, key_block, value_block, allowed):
    scores = jnp.einsum(
        "qkgd,nkd->kgqn", grouped_queries, key_block, preferred_element_type=jnp.float32
    ) / math.sqrt(grouped_queries.shape[-1])
    if allowed is not None:
        scores = jnp.where(allowed[None, None], scores, -jnp.inf)
    peak = jnp.max(scores, axis=-1)
    weights = jnp.exp(scores - peak[..., None])
    weight_sum = jnp.sum(weights, axis=-1)
    summed = jnp.einsum(
        "kgqn,nkd->kgqd",
        weights.astype(jnp.bfloat16),
        value_block,
        preferred_element_type=jnp.float32,
    )
    return jnp.concatenate([summed, peak[..., None], weight_sum[..., None]], axis=-1)


def combine_states(former, latter):
    head_dim = former.shape[-1] - 2
    peak = jnp.maximum(former[..., head_dim], latter[..., head_dim])
    scale_former = jnp.exp(former[..., head_dim] - peak)
    scale_latter = jnp.exp(latter[..., head_dim] - peak)
    summed = (
        former[..., :head_dim] * scale_former[..., None]
        + latter[..., :head_dim] * scale_latter[..., None]
    )
    weight_sum = (
        former[..., head_dim + 1] * scale_former + latter[..., head_dim + 1] * scale_latter
    )
    return jnp.concatenate([summed, peak[..., None], weight_sum[..., None]], axis=-1)


def layer(
    hidden_in,
    attn_gain,
    w_query,
    w_key,
    w_value,
    w_out,
    mlp_gain,
    w_gate,
    w_up,
    w_down,
    prefix_kv,
    suffix_lengths,
    prefix_owner,
):
    slots_here = hidden_in.shape[0]
    head_dim = HEAD_DIM
    kv_heads = w_key.shape[1] // head_dim
    q_heads = w_query.shape[1] // head_dim
    group = q_heads // kv_heads
    block_len = prefix_kv.shape[0]
    unit_count = w_gate.shape[1]
    width_part = w_gate.shape[0]
    n_az = lax.axis_size("az")
    n_rc = lax.axis_size("rc")
    n_mlp = lax.axis_size("mlp")
    az_index = lax.axis_index("az")
    rc_index = lax.axis_index("rc")
    req_index = (lax.axis_index("ax") * n_az + az_index) * n_rc + rc_index
    mlp_index = lax.axis_index("mlp")

    own = (jnp.concatenate([w_gate, w_up], axis=1), w_down)
    from_left = lax.ppermute(own, "mlp", [(i, (i + 1) % n_mlp) for i in range(n_mlp)])
    from_right = lax.ppermute(own, "mlp", [(i, (i - 1) % n_mlp) for i in range(n_mlp)])
    half_gu = width_part // 2
    half_wd = unit_count // 2
    relay_a = lax.ppermute(
        (from_left[0][:half_gu], from_left[1][:half_wd]),
        "mlp",
        [(i, (i + 1) % n_mlp) for i in range(n_mlp)],
    )
    relay_b = lax.ppermute(
        (from_right[0][half_gu:], from_right[1][half_wd:]),
        "mlp",
        [(i, (i - 1) % n_mlp) for i in range(n_mlp)],
    )
    across = (
        jnp.concatenate([relay_a[0], relay_b[0]], axis=0),
        jnp.concatenate([relay_a[1], relay_b[1]], axis=0),
    )
    gate_up_ring = jnp.stack([own[0], from_left[0], across[0], from_right[0]])
    down_ring = jnp.stack([own[1], from_left[1], across[1], from_right[1]], axis=1)
    down_ring = down_ring.reshape(unit_count, n_mlp * width_part)
    gate_up_other, down_other = swap_with_partner((gate_up_ring, down_ring), "rc", n_rc)
    gate_up_pair = (gate_up_ring, gate_up_other)
    down_pair = (down_ring, down_other)
    quarter_of = [(mlp_index - ring) % n_mlp for ring in range(n_mlp)]

    request_of, live, positions = slot_layout(suffix_lengths[0], slots_here)
    hidden_f = hidden_in.astype(jnp.float32)
    normed = rms_norm(hidden_f, attn_gain).astype(jnp.bfloat16)
    query_rows = rope(
        jnp.dot(normed, w_query, preferred_element_type=jnp.float32).reshape(
            slots_here, q_heads, head_dim
        ),
        positions,
    ).astype(jnp.bfloat16)
    key_rows = rope(
        jnp.dot(normed, w_key, preferred_element_type=jnp.float32).reshape(
            slots_here, kv_heads, head_dim
        ),
        positions,
    ).astype(jnp.bfloat16)
    value_rows = (
        jnp.dot(normed, w_value, preferred_element_type=jnp.float32)
        .astype(jnp.bfloat16)
        .reshape(slots_here, kv_heads, head_dim)
    )
    grouped_queries = query_rows.reshape(slots_here, kv_heads, group, head_dim)

    place = req_index % GSPAN
    group_id = req_index // GSPAN
    owners = lax.dynamic_index_in_dim(prefix_owner, group_id, 0, keepdims=False)
    quarter = jnp.sum(jnp.where(owners == place, jnp.arange(GSPAN, dtype=jnp.int32), 0))
    prefix_pos = quarter * block_len + jnp.arange(block_len, dtype=jnp.int32)
    stored_keys = rope(
        prefix_kv[:, 0].reshape(block_len, kv_heads, head_dim).astype(jnp.float32), prefix_pos
    ).astype(jnp.bfloat16)
    stored_values = prefix_kv[:, 1].reshape(block_len, kv_heads, head_dim)

    z_bit = az_index % 2
    core_other = swap_with_partner(grouped_queries, "rc", n_rc)
    pair = jnp.where(
        rc_index == 0,
        jnp.stack([grouped_queries, core_other]),
        jnp.stack([core_other, grouped_queries]),
    )
    z_other = swap_with_partner(pair, "az", n_az)
    group_queries = jnp.where(
        z_bit == 0, jnp.concatenate([pair, z_other]), jnp.concatenate([z_other, pair])
    )
    runs = group_queries.shape[0]
    states = partial_attention(
        group_queries.reshape(runs * slots_here, kv_heads, group, head_dim),
        stored_keys,
        stored_values,
        None,
    )
    states = states.reshape(kv_heads, group, runs, slots_here, head_dim + 2)
    keep = lax.dynamic_slice_in_dim(states, z_bit * 2, 2, 2)
    send = lax.dynamic_slice_in_dim(states, (1 - z_bit) * 2, 2, 2)
    states = combine_states(keep, swap_with_partner(send, "az", n_az))
    keep = lax.dynamic_slice_in_dim(states, rc_index, 1, 2)
    send = lax.dynamic_slice_in_dim(states, 1 - rc_index, 1, 2)
    prefix_state = combine_states(keep, swap_with_partner(send, "rc", n_rc))[:, :, 0]

    slot_ids = jnp.arange(slots_here, dtype=jnp.int32)
    allowed = (request_of[:, None] == request_of[None, :]) & (
        slot_ids[None, :] <= slot_ids[:, None]
    )
    suffix_state = partial_attention(grouped_queries, key_rows, value_rows, allowed)
    merged = combine_states(prefix_state, suffix_state)
    attended = (
        jnp.transpose(merged[..., :head_dim] / merged[..., head_dim + 1 :], (2, 0, 1, 3))
        .reshape(slots_here, q_heads * head_dim)
        .astype(jnp.bfloat16)
    )

    head_terms = jnp.dot(attended, w_out, preferred_element_type=jnp.float32)
    head_rows = lax.psum_scatter(head_terms, "mlp", scatter_dimension=0, tiled=True)
    rows_here = slots_here // n_mlp
    row_start = mlp_index * rows_here
    hidden_rows = lax.dynamic_slice_in_dim(hidden_f, row_start, rows_here, 0)
    live_rows = lax.dynamic_slice_in_dim(live, row_start, rows_here, 0)
    residual = (hidden_rows + head_rows).astype(jnp.bfloat16)
    normed_mlp = rms_norm(residual.astype(jnp.float32), mlp_gain).astype(jnp.bfloat16)

    n_ax = lax.axis_size("ax")
    tokens = gather_plane(normed_mlp, n_ax, n_az)
    tokens_ring = jnp.concatenate(
        [
            lax.dynamic_slice_in_dim(tokens, quarter_of[ring] * width_part, width_part, 1)
            for ring in range(n_mlp)
        ],
        axis=1,
    )
    acts = []
    for core in range(n_rc):
        weights_here = gate_up_pair[core].reshape(n_mlp * width_part, 2 * unit_count)
        gate_up = jnp.dot(tokens_ring, weights_here, preferred_element_type=jnp.float32)
        gate = gate_up[:, :unit_count]
        up_part = gate_up[:, unit_count:]
        acts.append((jax.nn.silu(gate) * up_part).astype(jnp.bfloat16))
    down_sum = None
    for core in range(n_rc):
        term = jnp.dot(acts[core], down_pair[core], preferred_element_type=jnp.float32)
        term = term.astype(jnp.bfloat16).astype(jnp.float32)
        down_sum = term if down_sum is None else down_sum + term
    down = reduce_plane(down_sum.astype(jnp.bfloat16), n_ax, n_az)
    down = down.reshape(rows_here, n_mlp, width_part)
    natural = jnp.stack([(mlp_index - j) % n_mlp for j in range(n_mlp)])
    down = jnp.take(down, natural, axis=1).reshape(rows_here, n_mlp * width_part)
    down = down.astype(jnp.float32)
    out_rows = jnp.where(
        live_rows[:, None], residual.astype(jnp.float32) + down, 0.0
    ).astype(jnp.bfloat16)
    hidden_out = lax.all_to_all(out_rows, "mlp", 1, 0, tiled=True)

    stacked_kv = jnp.stack(
        [
            key_rows.reshape(slots_here, kv_heads * head_dim),
            value_rows.reshape(slots_here, kv_heads * head_dim),
        ],
        axis=1,
    )
    suffix_kv = jnp.where(live[:, None, None], stacked_kv, jnp.zeros_like(stacked_kv))
    return (hidden_out, suffix_kv)


def solution(mesh):
    req_size, mlp_size = mesh.devices.shape
    x_size = req_size // 8
    view = Mesh(
        np.asarray(mesh.devices).reshape(x_size, 4, 2, mlp_size), ("ax", "az", "rc", "mlp")
    )
    placed = (
        P(REQ, None),
        P(),
        P(None, "mlp"),
        P(None, "mlp"),
        P(None, "mlp"),
        P("mlp", None),
        P(),
        P("mlp", REQ),
        P("mlp", REQ),
        P(REQ, "mlp"),
        P(REQ, None, "mlp"),
        P(REQ, None),
        P(),
    )
    return jax.shard_map(
        layer,
        mesh=view,
        in_specs=placed,
        out_specs=(P(REQ, "mlp"), P(REQ, None, "mlp")),
        check_vma=False,
    )
```

```python
import math

import jax
import jax.numpy as jnp
import numpy as np
from jax import lax
from jax.sharding import Mesh
from jax.sharding import PartitionSpec as P


HEAD_DIM = 128
PREFIX = 8192
GSPAN = 4

REQ = ("ax", "az", "rc")

rope_base = 500000.0
eps = 1e-05


def shifted(value, axis, size, shift):
    return lax.ppermute(value, axis, [(i, (i + shift) % size) for i in range(size)])


def gather_plane(rows, n_ax, n_az):
    half = rows.shape[1] // 2
    part_a = rows[:, :half]
    part_b = rows[:, half:]
    a_z = jnp.stack([part_a] + [shifted(part_a, "az", n_az, d) for d in range(1, n_az)])
    b_x = jnp.stack([part_b] + [shifted(part_b, "ax", n_ax, d) for d in range(1, n_ax)])
    a_zx = jnp.stack([a_z] + [shifted(a_z, "ax", n_ax, d) for d in range(1, n_ax)])
    b_xz = jnp.stack([b_x] + [shifted(b_x, "az", n_az, d) for d in range(1, n_az)])
    return jnp.concatenate(
        [a_zx.reshape(-1, half), jnp.swapaxes(b_xz, 0, 1).reshape(-1, half)], axis=1
    )


def reduce_plane(blocks, n_ax, n_az):
    rows = blocks.shape[0] // (n_ax * n_az)
    half = blocks.shape[1] // 2
    blocks = blocks.reshape(n_ax, n_az, rows, 2 * half)
    part_a = blocks[..., :half]
    part_b = blocks[..., half:]

    def fold(stack, axis, size):
        total = stack[0].astype(jnp.float32)
        for d in range(1, size):
            total = total + shifted(stack[d], axis, size, -d).astype(jnp.float32)
        return total

    a_1 = fold(part_a, "ax", n_ax).astype(jnp.bfloat16)
    a_2 = fold(a_1, "az", n_az)
    b_1 = fold(jnp.swapaxes(part_b, 0, 1), "az", n_az).astype(jnp.bfloat16)
    b_2 = fold(b_1, "ax", n_ax)
    return jnp.concatenate([a_2, b_2], axis=1)


def swap_with_partner(value, axis, size):
    return lax.ppermute(value, axis, [(source, source ^ 1) for source in range(size)])


def rope(values, positions):
    half = values.shape[-1] // 2
    freq = rope_base ** (-jnp.arange(half, dtype=jnp.float32) * 2.0 / values.shape[-1])
    angle = positions.astype(jnp.float32)[:, None] * freq[None, :]
    cosine = jnp.cos(angle)[:, None, :]
    sine = jnp.sin(angle)[:, None, :]
    former = values[..., :half]
    latter = values[..., half:]
    return jnp.concatenate(
        [former * cosine - latter * sine, latter * cosine + former * sine], axis=-1
    )


def rms_norm(values, gain):
    return (
        values
        * lax.rsqrt(jnp.mean(values * values, axis=-1, keepdims=True) + eps)
        * gain.astype(jnp.float32)
    )


def slot_layout(lengths, slot_count):
    ends = jnp.cumsum(lengths)
    starts = ends - lengths
    slot_ids = jnp.arange(slot_count, dtype=jnp.int32)
    request_of = jnp.sum((slot_ids[:, None] >= ends[None, :]).astype(jnp.int32), axis=1)
    picks = (request_of[:, None] == jnp.arange(lengths.shape[0], dtype=jnp.int32)[None, :]).astype(
        jnp.int32
    )
    start_of = jnp.sum(picks * starts[None, :], axis=1)
    positions = PREFIX + slot_ids - start_of
    return (request_of, request_of < lengths.shape[0], positions)


def partial_attention(grouped_queries, key_block, value_block, allowed):
    scores = jnp.einsum(
        "qkgd,nkd->kgqn", grouped_queries, key_block, preferred_element_type=jnp.float32
    ) / math.sqrt(grouped_queries.shape[-1])
    if allowed is not None:
        scores = jnp.where(allowed[None, None], scores, -jnp.inf)
    peak = jnp.max(scores, axis=-1)
    weights = jnp.exp(scores - peak[..., None])
    weight_sum = jnp.sum(weights, axis=-1)
    summed = jnp.einsum(
        "kgqn,nkd->kgqd",
        weights.astype(jnp.bfloat16),
        value_block,
        preferred_element_type=jnp.float32,
    )
    return jnp.concatenate([summed, peak[..., None], weight_sum[..., None]], axis=-1)


def combine_states(former, latter):
    head_dim = former.shape[-1] - 2
    peak = jnp.maximum(former[..., head_dim], latter[..., head_dim])
    scale_former = jnp.exp(former[..., head_dim] - peak)
    scale_latter = jnp.exp(latter[..., head_dim] - peak)
    summed = (
        former[..., :head_dim] * scale_former[..., None]
        + latter[..., :head_dim] * scale_latter[..., None]
    )
    weight_sum = (
        former[..., head_dim + 1] * scale_former + latter[..., head_dim + 1] * scale_latter
    )
    return jnp.concatenate([summed, peak[..., None], weight_sum[..., None]], axis=-1)


def layer(
    hidden_in,
    attn_gain,
    w_query,
    w_key,
    w_value,
    w_out,
    mlp_gain,
    w_gate,
    w_up,
    w_down,
    prefix_kv,
    suffix_lengths,
    prefix_owner,
):
    slots_here = hidden_in.shape[0]
    head_dim = HEAD_DIM
    kv_heads = w_key.shape[1] // head_dim
    q_heads = w_query.shape[1] // head_dim
    group = q_heads // kv_heads
    block_len = prefix_kv.shape[0]
    unit_count = w_gate.shape[1]
    width_part = w_gate.shape[0]
    n_az = lax.axis_size("az")
    n_rc = lax.axis_size("rc")
    n_mlp = lax.axis_size("mlp")
    az_index = lax.axis_index("az")
    rc_index = lax.axis_index("rc")
    req_index = (lax.axis_index("ax") * n_az + az_index) * n_rc + rc_index
    mlp_index = lax.axis_index("mlp")

    own = (jnp.concatenate([w_gate, w_up], axis=1), w_down)
    from_left = lax.ppermute(own, "mlp", [(i, (i + 1) % n_mlp) for i in range(n_mlp)])
    from_right = lax.ppermute(own, "mlp", [(i, (i - 1) % n_mlp) for i in range(n_mlp)])
    half_gu = width_part // 2
    half_wd = unit_count // 2
    relay_a = lax.ppermute(
        (from_left[0][:half_gu], from_left[1][:half_wd]),
        "mlp",
        [(i, (i + 1) % n_mlp) for i in range(n_mlp)],
    )
    relay_b = lax.ppermute(
        (from_right[0][half_gu:], from_right[1][half_wd:]),
        "mlp",
        [(i, (i - 1) % n_mlp) for i in range(n_mlp)],
    )
    across = (
        jnp.concatenate([relay_a[0], relay_b[0]], axis=0),
        jnp.concatenate([relay_a[1], relay_b[1]], axis=0),
    )
    gate_up_ring = jnp.stack([own[0], from_left[0], across[0], from_right[0]])
    down_ring = jnp.stack([own[1], from_left[1], across[1], from_right[1]], axis=1)
    down_ring = down_ring.reshape(unit_count, n_mlp * width_part)
    gate_up_other, down_other = swap_with_partner((gate_up_ring, down_ring), "rc", n_rc)
    gate_up_pair = (gate_up_ring, gate_up_other)
    down_pair = (down_ring, down_other)
    quarter_of = [(mlp_index - ring) % n_mlp for ring in range(n_mlp)]

    request_of, live, positions = slot_layout(suffix_lengths[0], slots_here)
    hidden_f = hidden_in.astype(jnp.float32)
    normed = rms_norm(hidden_f, attn_gain).astype(jnp.bfloat16)
    query_rows = rope(
        jnp.dot(normed, w_query, preferred_element_type=jnp.float32).reshape(
            slots_here, q_heads, head_dim
        ),
        positions,
    ).astype(jnp.bfloat16)
    key_rows = rope(
        jnp.dot(normed, w_key, preferred_element_type=jnp.float32).reshape(
            slots_here, kv_heads, head_dim
        ),
        positions,
    ).astype(jnp.bfloat16)
    value_rows = (
        jnp.dot(normed, w_value, preferred_element_type=jnp.float32)
        .astype(jnp.bfloat16)
        .reshape(slots_here, kv_heads, head_dim)
    )
    grouped_queries = query_rows.reshape(slots_here, kv_heads, group, head_dim)

    place = req_index % GSPAN
    group_id = req_index // GSPAN
    owners = lax.dynamic_index_in_dim(prefix_owner, group_id, 0, keepdims=False)
    quarter = jnp.sum(jnp.where(owners == place, jnp.arange(GSPAN, dtype=jnp.int32), 0))
    prefix_pos = quarter * block_len + jnp.arange(block_len, dtype=jnp.int32)
    stored_keys = rope(
        prefix_kv[:, 0].reshape(block_len, kv_heads, head_dim).astype(jnp.float32), prefix_pos
    ).astype(jnp.bfloat16)
    stored_values = prefix_kv[:, 1].reshape(block_len, kv_heads, head_dim)

    z_bit = az_index % 2
    core_other = swap_with_partner(grouped_queries, "rc", n_rc)
    pair = jnp.where(
        rc_index == 0,
        jnp.stack([grouped_queries, core_other]),
        jnp.stack([core_other, grouped_queries]),
    )
    z_other = swap_with_partner(pair, "az", n_az)
    group_queries = jnp.where(
        z_bit == 0, jnp.concatenate([pair, z_other]), jnp.concatenate([z_other, pair])
    )
    runs = group_queries.shape[0]
    states = partial_attention(
        group_queries.reshape(runs * slots_here, kv_heads, group, head_dim),
        stored_keys,
        stored_values,
        None,
    )
    states = states.reshape(kv_heads, group, runs, slots_here, head_dim + 2)
    keep = lax.dynamic_slice_in_dim(states, z_bit * 2, 2, 2)
    send = lax.dynamic_slice_in_dim(states, (1 - z_bit) * 2, 2, 2)
    states = combine_states(keep, swap_with_partner(send, "az", n_az))
    keep = lax.dynamic_slice_in_dim(states, rc_index, 1, 2)
    send = lax.dynamic_slice_in_dim(states, 1 - rc_index, 1, 2)
    prefix_state = combine_states(keep, swap_with_partner(send, "rc", n_rc))[:, :, 0]

    slot_ids = jnp.arange(slots_here, dtype=jnp.int32)
    allowed = (request_of[:, None] == request_of[None, :]) & (
        slot_ids[None, :] <= slot_ids[:, None]
    )
    suffix_state = partial_attention(grouped_queries, key_rows, value_rows, allowed)
    merged = combine_states(prefix_state, suffix_state)
    attended = (
        jnp.transpose(merged[..., :head_dim] / merged[..., head_dim + 1 :], (2, 0, 1, 3))
        .reshape(slots_here, q_heads * head_dim)
        .astype(jnp.bfloat16)
    )

    head_terms = jnp.dot(attended, w_out, preferred_element_type=jnp.float32)
    rows_here = slots_here // n_mlp
    head_rows = lax.dynamic_slice_in_dim(head_terms, mlp_index * rows_here, rows_here, 0)
    for shift in range(1, n_mlp):
        target = (mlp_index + shift) % n_mlp
        outgoing = lax.dynamic_slice_in_dim(head_terms, target * rows_here, rows_here, 0)
        head_rows = head_rows + shifted(outgoing, "mlp", n_mlp, shift)
    row_start = mlp_index * rows_here
    hidden_rows = lax.dynamic_slice_in_dim(hidden_f, row_start, rows_here, 0)
    live_rows = lax.dynamic_slice_in_dim(live, row_start, rows_here, 0)
    residual = (hidden_rows + head_rows).astype(jnp.bfloat16)
    normed_mlp = rms_norm(residual.astype(jnp.float32), mlp_gain).astype(jnp.bfloat16)

    n_ax = lax.axis_size("ax")
    tokens = gather_plane(normed_mlp, n_ax, n_az)
    tokens_ring = jnp.concatenate(
        [
            lax.dynamic_slice_in_dim(tokens, quarter_of[ring] * width_part, width_part, 1)
            for ring in range(n_mlp)
        ],
        axis=1,
    )
    acts = []
    for core in range(n_rc):
        weights_here = gate_up_pair[core].reshape(n_mlp * width_part, 2 * unit_count)
        gate_up = jnp.dot(tokens_ring, weights_here, preferred_element_type=jnp.float32)
        gate = gate_up[:, :unit_count]
        up_part = gate_up[:, unit_count:]
        acts.append((jax.nn.silu(gate) * up_part).astype(jnp.bfloat16))
    down_sum = None
    for core in range(n_rc):
        term = jnp.dot(acts[core], down_pair[core], preferred_element_type=jnp.float32)
        term = term.astype(jnp.bfloat16).astype(jnp.float32)
        down_sum = term if down_sum is None else down_sum + term
    down = reduce_plane(down_sum.astype(jnp.bfloat16), n_ax, n_az)
    down = down.reshape(rows_here, n_mlp, width_part)
    natural = jnp.stack([(mlp_index - j) % n_mlp for j in range(n_mlp)])
    down = jnp.take(down, natural, axis=1).reshape(rows_here, n_mlp * width_part)
    down = down.astype(jnp.float32)
    out_rows = jnp.where(
        live_rows[:, None], residual.astype(jnp.float32) + down, 0.0
    ).astype(jnp.bfloat16)
    hidden_out = lax.all_to_all(out_rows, "mlp", 1, 0, tiled=True)

    stacked_kv = jnp.stack(
        [
            key_rows.reshape(slots_here, kv_heads * head_dim),
            value_rows.reshape(slots_here, kv_heads * head_dim),
        ],
        axis=1,
    )
    suffix_kv = jnp.where(live[:, None, None], stacked_kv, jnp.zeros_like(stacked_kv))
    return (hidden_out, suffix_kv)


def solution(mesh):
    req_size, mlp_size = mesh.devices.shape
    x_size = req_size // 8
    view = Mesh(
        np.asarray(mesh.devices).reshape(x_size, 4, 2, mlp_size), ("ax", "az", "rc", "mlp")
    )
    placed = (
        P(REQ, None),
        P(),
        P(None, "mlp"),
        P(None, "mlp"),
        P(None, "mlp"),
        P("mlp", None),
        P(),
        P("mlp", REQ),
        P("mlp", REQ),
        P(REQ, "mlp"),
        P(REQ, None, "mlp"),
        P(REQ, None),
        P(),
    )
    return jax.shard_map(
        layer,
        mesh=view,
        in_specs=placed,
        out_specs=(P(REQ, "mlp"), P(REQ, None, "mlp")),
        check_vma=False,
    )
```

```python
import math

import jax
import jax.numpy as jnp
import numpy as np
from jax import lax
from jax.sharding import Mesh
from jax.sharding import PartitionSpec as P


HEAD_DIM = 128
PREFIX = 8192
GSPAN = 4

REQ = ("ax", "az", "rc")

rope_base = 500000.0
eps = 1e-05


def shifted(value, axis, size, shift):
    return lax.ppermute(value, axis, [(i, (i + shift) % size) for i in range(size)])


def gather_plane(rows, n_ax, n_az):
    half = rows.shape[1] // 2
    part_a = rows[:, :half]
    part_b = rows[:, half:]
    a_z = jnp.stack([part_a] + [shifted(part_a, "az", n_az, d) for d in range(1, n_az)])
    b_x = jnp.stack([part_b] + [shifted(part_b, "ax", n_ax, d) for d in range(1, n_ax)])
    a_zx = jnp.stack([a_z] + [shifted(a_z, "ax", n_ax, d) for d in range(1, n_ax)])
    b_xz = jnp.stack([b_x] + [shifted(b_x, "az", n_az, d) for d in range(1, n_az)])
    return jnp.concatenate(
        [a_zx.reshape(-1, half), jnp.swapaxes(b_xz, 0, 1).reshape(-1, half)], axis=1
    )


def reduce_plane(blocks, n_ax, n_az):
    rows = blocks.shape[0] // (n_ax * n_az)
    half = blocks.shape[1] // 2
    blocks = blocks.reshape(n_ax, n_az, rows, 2 * half)
    part_a = blocks[..., :half]
    part_b = blocks[..., half:]

    def fold(stack, axis, size):
        total = stack[0].astype(jnp.float32)
        for d in range(1, size):
            total = total + shifted(stack[d], axis, size, -d).astype(jnp.float32)
        return total

    a_1 = fold(part_a, "ax", n_ax).astype(jnp.bfloat16)
    a_2 = fold(a_1, "az", n_az)
    b_1 = fold(jnp.swapaxes(part_b, 0, 1), "az", n_az).astype(jnp.bfloat16)
    b_2 = fold(b_1, "ax", n_ax)
    return jnp.concatenate([a_2, b_2], axis=1)


def swap_with_partner(value, axis, size):
    return lax.ppermute(value, axis, [(source, source ^ 1) for source in range(size)])


def rope(values, positions):
    half = values.shape[-1] // 2
    freq = rope_base ** (-jnp.arange(half, dtype=jnp.float32) * 2.0 / values.shape[-1])
    angle = positions.astype(jnp.float32)[:, None] * freq[None, :]
    cosine = jnp.cos(angle)[:, None, :]
    sine = jnp.sin(angle)[:, None, :]
    former = values[..., :half]
    latter = values[..., half:]
    return jnp.concatenate(
        [former * cosine - latter * sine, latter * cosine + former * sine], axis=-1
    )


def rms_norm(values, gain):
    return (
        values
        * lax.rsqrt(jnp.mean(values * values, axis=-1, keepdims=True) + eps)
        * gain.astype(jnp.float32)
    )


def slot_layout(lengths, slot_count):
    ends = jnp.cumsum(lengths)
    starts = ends - lengths
    slot_ids = jnp.arange(slot_count, dtype=jnp.int32)
    request_of = jnp.sum((slot_ids[:, None] >= ends[None, :]).astype(jnp.int32), axis=1)
    picks = (request_of[:, None] == jnp.arange(lengths.shape[0], dtype=jnp.int32)[None, :]).astype(
        jnp.int32
    )
    start_of = jnp.sum(picks * starts[None, :], axis=1)
    positions = PREFIX + slot_ids - start_of
    return (request_of, request_of < lengths.shape[0], positions)


def partial_attention(grouped_queries, key_block, value_block, allowed):
    scores = jnp.einsum(
        "qkgd,nkd->kgqn", grouped_queries, key_block, preferred_element_type=jnp.float32
    ) / math.sqrt(grouped_queries.shape[-1])
    if allowed is not None:
        scores = jnp.where(allowed[None, None], scores, -jnp.inf)
    peak = jnp.max(scores, axis=-1)
    weights = jnp.exp(scores - peak[..., None])
    weight_sum = jnp.sum(weights, axis=-1)
    summed = jnp.einsum(
        "kgqn,nkd->kgqd",
        weights.astype(jnp.bfloat16),
        value_block,
        preferred_element_type=jnp.float32,
    )
    return jnp.concatenate([summed, peak[..., None], weight_sum[..., None]], axis=-1)


def combine_states(former, latter):
    head_dim = former.shape[-1] - 2
    peak = jnp.maximum(former[..., head_dim], latter[..., head_dim])
    scale_former = jnp.exp(former[..., head_dim] - peak)
    scale_latter = jnp.exp(latter[..., head_dim] - peak)
    summed = (
        former[..., :head_dim] * scale_former[..., None]
        + latter[..., :head_dim] * scale_latter[..., None]
    )
    weight_sum = (
        former[..., head_dim + 1] * scale_former + latter[..., head_dim + 1] * scale_latter
    )
    return jnp.concatenate([summed, peak[..., None], weight_sum[..., None]], axis=-1)


def layer(
    hidden_in,
    attn_gain,
    w_query,
    w_key,
    w_value,
    w_out,
    mlp_gain,
    w_gate,
    w_up,
    w_down,
    prefix_kv,
    suffix_lengths,
    prefix_owner,
):
    slots_here = hidden_in.shape[0]
    head_dim = HEAD_DIM
    kv_heads = w_key.shape[1] // head_dim
    q_heads = w_query.shape[1] // head_dim
    group = q_heads // kv_heads
    block_len = prefix_kv.shape[0]
    unit_count = w_gate.shape[1]
    width_part = w_gate.shape[0]
    n_az = lax.axis_size("az")
    n_rc = lax.axis_size("rc")
    n_mlp = lax.axis_size("mlp")
    az_index = lax.axis_index("az")
    rc_index = lax.axis_index("rc")
    req_index = (lax.axis_index("ax") * n_az + az_index) * n_rc + rc_index
    mlp_index = lax.axis_index("mlp")

    own = (jnp.concatenate([w_gate, w_up], axis=1), w_down)
    left_gu = shifted(own[0], "mlp", n_mlp, 1)
    right_gu = shifted(own[0], "mlp", n_mlp, -1)
    left_wd = shifted(own[1], "mlp", n_mlp, 1)
    right_wd = shifted(own[1], "mlp", n_mlp, -1)
    from_left = (left_gu, left_wd)
    from_right = (right_gu, right_wd)
    half_gu = width_part // 2
    half_wd = unit_count // 2
    relay_a = lax.ppermute(
        (from_left[0][:half_gu], from_left[1][:half_wd]),
        "mlp",
        [(i, (i + 1) % n_mlp) for i in range(n_mlp)],
    )
    relay_b = lax.ppermute(
        (from_right[0][half_gu:], from_right[1][half_wd:]),
        "mlp",
        [(i, (i - 1) % n_mlp) for i in range(n_mlp)],
    )
    across = (
        jnp.concatenate([relay_a[0], relay_b[0]], axis=0),
        jnp.concatenate([relay_a[1], relay_b[1]], axis=0),
    )
    gate_up_ring = jnp.stack([own[0], from_left[0], across[0], from_right[0]])
    down_ring = jnp.stack([own[1], from_left[1], across[1], from_right[1]], axis=1)
    down_ring = down_ring.reshape(unit_count, n_mlp * width_part)
    gate_up_other, down_other = swap_with_partner((gate_up_ring, down_ring), "rc", n_rc)
    gate_up_pair = (gate_up_ring, gate_up_other)
    down_pair = (down_ring, down_other)
    quarter_of = [(mlp_index - ring) % n_mlp for ring in range(n_mlp)]

    request_of, live, positions = slot_layout(suffix_lengths[0], slots_here)
    hidden_f = hidden_in.astype(jnp.float32)
    normed = rms_norm(hidden_f, attn_gain).astype(jnp.bfloat16)
    query_rows = rope(
        jnp.dot(normed, w_query, preferred_element_type=jnp.float32).reshape(
            slots_here, q_heads, head_dim
        ),
        positions,
    ).astype(jnp.bfloat16)
    key_rows = rope(
        jnp.dot(normed, w_key, preferred_element_type=jnp.float32).reshape(
            slots_here, kv_heads, head_dim
        ),
        positions,
    ).astype(jnp.bfloat16)
    value_rows = (
        jnp.dot(normed, w_value, preferred_element_type=jnp.float32)
        .astype(jnp.bfloat16)
        .reshape(slots_here, kv_heads, head_dim)
    )
    grouped_queries = query_rows.reshape(slots_here, kv_heads, group, head_dim)

    place = req_index % GSPAN
    group_id = req_index // GSPAN
    owners = lax.dynamic_index_in_dim(prefix_owner, group_id, 0, keepdims=False)
    quarter = jnp.sum(jnp.where(owners == place, jnp.arange(GSPAN, dtype=jnp.int32), 0))
    prefix_pos = quarter * block_len + jnp.arange(block_len, dtype=jnp.int32)
    stored_keys = rope(
        prefix_kv[:, 0].reshape(block_len, kv_heads, head_dim).astype(jnp.float32), prefix_pos
    ).astype(jnp.bfloat16)
    stored_values = prefix_kv[:, 1].reshape(block_len, kv_heads, head_dim)

    z_bit = az_index % 2
    core_other = swap_with_partner(grouped_queries, "rc", n_rc)
    pair = jnp.where(
        rc_index == 0,
        jnp.stack([grouped_queries, core_other]),
        jnp.stack([core_other, grouped_queries]),
    )
    z_other = swap_with_partner(pair, "az", n_az)
    group_queries = jnp.where(
        z_bit == 0, jnp.concatenate([pair, z_other]), jnp.concatenate([z_other, pair])
    )
    runs = group_queries.shape[0]
    states = partial_attention(
        group_queries.reshape(runs * slots_here, kv_heads, group, head_dim),
        stored_keys,
        stored_values,
        None,
    )
    states = states.reshape(kv_heads, group, runs, slots_here, head_dim + 2)
    keep = lax.dynamic_slice_in_dim(states, z_bit * 2, 2, 2)
    send = lax.dynamic_slice_in_dim(states, (1 - z_bit) * 2, 2, 2)
    from_z = swap_with_partner(send, "az", n_az)
    states = combine_states(keep, from_z)
    keep = lax.dynamic_slice_in_dim(states, rc_index, 1, 2)
    send = lax.dynamic_slice_in_dim(states, 1 - rc_index, 1, 2)
    prefix_state = combine_states(keep, swap_with_partner(send, "rc", n_rc))[:, :, 0]

    slot_ids = jnp.arange(slots_here, dtype=jnp.int32)
    allowed = (request_of[:, None] == request_of[None, :]) & (
        slot_ids[None, :] <= slot_ids[:, None]
    )
    suffix_state = partial_attention(grouped_queries, key_rows, value_rows, allowed)
    merged = combine_states(prefix_state, suffix_state)
    attended = (
        jnp.transpose(merged[..., :head_dim] / merged[..., head_dim + 1 :], (2, 0, 1, 3))
        .reshape(slots_here, q_heads * head_dim)
        .astype(jnp.bfloat16)
    )

    head_terms = jnp.dot(attended, w_out, preferred_element_type=jnp.float32)
    rows_here = slots_here // n_mlp
    head_rows = lax.dynamic_slice_in_dim(head_terms, mlp_index * rows_here, rows_here, 0)
    for shift in range(1, n_mlp):
        target = (mlp_index + shift) % n_mlp
        outgoing = lax.dynamic_slice_in_dim(head_terms, target * rows_here, rows_here, 0)
        head_rows = head_rows + shifted(outgoing, "mlp", n_mlp, shift)
    row_start = mlp_index * rows_here
    hidden_rows = lax.dynamic_slice_in_dim(hidden_f, row_start, rows_here, 0)
    live_rows = lax.dynamic_slice_in_dim(live, row_start, rows_here, 0)
    residual = (hidden_rows + head_rows).astype(jnp.bfloat16)
    normed_mlp = rms_norm(residual.astype(jnp.float32), mlp_gain).astype(jnp.bfloat16)

    n_ax = lax.axis_size("ax")
    tokens = gather_plane(normed_mlp, n_ax, n_az)
    tokens_ring = jnp.concatenate(
        [
            lax.dynamic_slice_in_dim(tokens, quarter_of[ring] * width_part, width_part, 1)
            for ring in range(n_mlp)
        ],
        axis=1,
    )
    acts = []
    for core in range(n_rc):
        weights_here = gate_up_pair[core].reshape(n_mlp * width_part, 2 * unit_count)
        gate_up = jnp.dot(tokens_ring, weights_here, preferred_element_type=jnp.float32)
        gate = gate_up[:, :unit_count]
        up_part = gate_up[:, unit_count:]
        acts.append((jax.nn.silu(gate) * up_part).astype(jnp.bfloat16))
    down_sum = None
    for core in range(n_rc):
        term = jnp.dot(acts[core], down_pair[core], preferred_element_type=jnp.float32)
        term = term.astype(jnp.bfloat16).astype(jnp.float32)
        down_sum = term if down_sum is None else down_sum + term
    down = reduce_plane(down_sum.astype(jnp.bfloat16), n_ax, n_az)
    down = down.reshape(rows_here, n_mlp, width_part)
    natural = jnp.stack([(mlp_index - j) % n_mlp for j in range(n_mlp)])
    down = jnp.take(down, natural, axis=1).reshape(rows_here, n_mlp * width_part)
    down = down.astype(jnp.float32)
    out_rows = jnp.where(
        live_rows[:, None], residual.astype(jnp.float32) + down, 0.0
    ).astype(jnp.bfloat16)
    hidden_out = lax.all_to_all(out_rows, "mlp", 1, 0, tiled=True)

    stacked_kv = jnp.stack(
        [
            key_rows.reshape(slots_here, kv_heads * head_dim),
            value_rows.reshape(slots_here, kv_heads * head_dim),
        ],
        axis=1,
    )
    suffix_kv = jnp.where(live[:, None, None], stacked_kv, jnp.zeros_like(stacked_kv))
    return (hidden_out, suffix_kv)


def solution(mesh):
    req_size, mlp_size = mesh.devices.shape
    x_size = req_size // 8
    view = Mesh(
        np.asarray(mesh.devices).reshape(x_size, 4, 2, mlp_size), ("ax", "az", "rc", "mlp")
    )
    placed = (
        P(REQ, None),
        P(),
        P(None, "mlp"),
        P(None, "mlp"),
        P(None, "mlp"),
        P("mlp", None),
        P(),
        P("mlp", REQ),
        P("mlp", REQ),
        P(REQ, "mlp"),
        P(REQ, None, "mlp"),
        P(REQ, None),
        P(),
    )
    return jax.shard_map(
        layer,
        mesh=view,
        in_specs=placed,
        out_specs=(P(REQ, "mlp"), P(REQ, None, "mlp")),
        check_vma=False,
    )
```

```python
import math

import jax
import jax.numpy as jnp
import numpy as np
from jax import lax
from jax.sharding import Mesh
from jax.sharding import PartitionSpec as P


HEAD_DIM = 128
PREFIX = 8192
GSPAN = 4

REQ = ("ax", "az", "rc")

rope_base = 500000.0
eps = 1e-05


def shifted(value, axis, size, shift):
    return lax.ppermute(value, axis, [(i, (i + shift) % size) for i in range(size)])


def gather_plane(rows, n_ax, n_az):
    half = rows.shape[1] // 2
    part_a = rows[:, :half]
    part_b = rows[:, half:]
    a_z = jnp.stack([part_a] + [shifted(part_a, "az", n_az, d) for d in range(1, n_az)])
    b_x = jnp.stack([part_b] + [shifted(part_b, "ax", n_ax, d) for d in range(1, n_ax)])
    a_zx = jnp.stack([a_z] + [shifted(a_z, "ax", n_ax, d) for d in range(1, n_ax)])
    b_xz = jnp.stack([b_x] + [shifted(b_x, "az", n_az, d) for d in range(1, n_az)])
    return jnp.concatenate(
        [a_zx.reshape(-1, half), jnp.swapaxes(b_xz, 0, 1).reshape(-1, half)], axis=1
    )


def reduce_plane(blocks, n_ax, n_az):
    rows = blocks.shape[0] // (n_ax * n_az)
    half = blocks.shape[1] // 2
    blocks = blocks.reshape(n_ax, n_az, rows, 2 * half)
    part_a = blocks[..., :half]
    part_b = blocks[..., half:]

    def fold(stack, axis, size):
        total = stack[0].astype(jnp.float32)
        for d in range(1, size):
            total = total + shifted(stack[d], axis, size, -d).astype(jnp.float32)
        return total

    a_1 = fold(part_a, "ax", n_ax).astype(jnp.bfloat16)
    a_2 = fold(a_1, "az", n_az)
    b_1 = fold(jnp.swapaxes(part_b, 0, 1), "az", n_az).astype(jnp.bfloat16)
    b_2 = fold(b_1, "ax", n_ax)
    return jnp.concatenate([a_2, b_2], axis=1)


def swap_with_partner(value, axis, size):
    return lax.ppermute(value, axis, [(source, source ^ 1) for source in range(size)])


def rope(values, positions):
    half = values.shape[-1] // 2
    freq = rope_base ** (-jnp.arange(half, dtype=jnp.float32) * 2.0 / values.shape[-1])
    angle = positions.astype(jnp.float32)[:, None] * freq[None, :]
    cosine = jnp.cos(angle)[:, None, :]
    sine = jnp.sin(angle)[:, None, :]
    former = values[..., :half]
    latter = values[..., half:]
    return jnp.concatenate(
        [former * cosine - latter * sine, latter * cosine + former * sine], axis=-1
    )


def rms_norm(values, gain):
    return (
        values
        * lax.rsqrt(jnp.mean(values * values, axis=-1, keepdims=True) + eps)
        * gain.astype(jnp.float32)
    )


def slot_layout(lengths, slot_count):
    ends = jnp.cumsum(lengths)
    starts = ends - lengths
    slot_ids = jnp.arange(slot_count, dtype=jnp.int32)
    request_of = jnp.sum((slot_ids[:, None] >= ends[None, :]).astype(jnp.int32), axis=1)
    picks = (request_of[:, None] == jnp.arange(lengths.shape[0], dtype=jnp.int32)[None, :]).astype(
        jnp.int32
    )
    start_of = jnp.sum(picks * starts[None, :], axis=1)
    positions = PREFIX + slot_ids - start_of
    return (request_of, request_of < lengths.shape[0], positions)


def partial_attention(grouped_queries, key_block, value_block, allowed):
    scores = jnp.einsum(
        "qkgd,nkd->kgqn", grouped_queries, key_block, preferred_element_type=jnp.float32
    ) / math.sqrt(grouped_queries.shape[-1])
    if allowed is not None:
        scores = jnp.where(allowed[None, None], scores, -jnp.inf)
    peak = jnp.max(scores, axis=-1)
    weights = jnp.exp(scores - peak[..., None])
    weight_sum = jnp.sum(weights, axis=-1)
    summed = jnp.einsum(
        "kgqn,nkd->kgqd",
        weights.astype(jnp.bfloat16),
        value_block,
        preferred_element_type=jnp.float32,
    )
    return jnp.concatenate([summed, peak[..., None], weight_sum[..., None]], axis=-1)


def combine_states(former, latter):
    head_dim = former.shape[-1] - 2
    peak = jnp.maximum(former[..., head_dim], latter[..., head_dim])
    scale_former = jnp.exp(former[..., head_dim] - peak)
    scale_latter = jnp.exp(latter[..., head_dim] - peak)
    summed = (
        former[..., :head_dim] * scale_former[..., None]
        + latter[..., :head_dim] * scale_latter[..., None]
    )
    weight_sum = (
        former[..., head_dim + 1] * scale_former + latter[..., head_dim + 1] * scale_latter
    )
    return jnp.concatenate([summed, peak[..., None], weight_sum[..., None]], axis=-1)


def layer(
    hidden_in,
    attn_gain,
    w_query,
    w_key,
    w_value,
    w_out,
    mlp_gain,
    w_gate,
    w_up,
    w_down,
    prefix_kv,
    suffix_lengths,
    prefix_owner,
):
    slots_here = hidden_in.shape[0]
    head_dim = HEAD_DIM
    kv_heads = w_key.shape[1] // head_dim
    q_heads = w_query.shape[1] // head_dim
    group = q_heads // kv_heads
    block_len = prefix_kv.shape[0]
    unit_count = w_gate.shape[1]
    width_part = w_gate.shape[0]
    n_az = lax.axis_size("az")
    n_rc = lax.axis_size("rc")
    n_mlp = lax.axis_size("mlp")
    az_index = lax.axis_index("az")
    rc_index = lax.axis_index("rc")
    req_index = (lax.axis_index("ax") * n_az + az_index) * n_rc + rc_index
    mlp_index = lax.axis_index("mlp")

    own = (jnp.concatenate([w_gate, w_up], axis=1), w_down)
    from_left = lax.ppermute(own, "mlp", [(i, (i + 1) % n_mlp) for i in range(n_mlp)])
    from_right = lax.ppermute(own, "mlp", [(i, (i - 1) % n_mlp) for i in range(n_mlp)])
    half_gu = width_part // 2
    half_wd = unit_count // 2
    relay_a = lax.ppermute(
        (from_left[0][:half_gu], from_left[1][:half_wd]),
        "mlp",
        [(i, (i + 1) % n_mlp) for i in range(n_mlp)],
    )
    relay_b = lax.ppermute(
        (from_right[0][half_gu:], from_right[1][half_wd:]),
        "mlp",
        [(i, (i - 1) % n_mlp) for i in range(n_mlp)],
    )
    across = (
        jnp.concatenate([relay_a[0], relay_b[0]], axis=0),
        jnp.concatenate([relay_a[1], relay_b[1]], axis=0),
    )
    gate_up_ring = jnp.stack([own[0], from_left[0], across[0], from_right[0]])
    down_ring = jnp.stack([own[1], from_left[1], across[1], from_right[1]], axis=1)
    down_ring = down_ring.reshape(unit_count, n_mlp * width_part)
    gate_up_other, down_other = swap_with_partner((gate_up_ring, down_ring), "rc", n_rc)
    gate_up_pair = (gate_up_ring, gate_up_other)
    down_pair = (down_ring, down_other)
    quarter_of = [(mlp_index - ring) % n_mlp for ring in range(n_mlp)]

    request_of, live, positions = slot_layout(suffix_lengths[0], slots_here)
    hidden_f = hidden_in.astype(jnp.float32)
    normed = rms_norm(hidden_f, attn_gain).astype(jnp.bfloat16)
    query_rows = rope(
        jnp.dot(normed, w_query, preferred_element_type=jnp.float32).reshape(
            slots_here, q_heads, head_dim
        ),
        positions,
    ).astype(jnp.bfloat16)
    key_rows = rope(
        jnp.dot(normed, w_key, preferred_element_type=jnp.float32).reshape(
            slots_here, kv_heads, head_dim
        ),
        positions,
    ).astype(jnp.bfloat16)
    value_rows = (
        jnp.dot(normed, w_value, preferred_element_type=jnp.float32)
        .astype(jnp.bfloat16)
        .reshape(slots_here, kv_heads, head_dim)
    )
    grouped_queries = query_rows.reshape(slots_here, kv_heads, group, head_dim)

    place = req_index % GSPAN
    group_id = req_index // GSPAN
    owners = lax.dynamic_index_in_dim(prefix_owner, group_id, 0, keepdims=False)
    quarter = jnp.sum(jnp.where(owners == place, jnp.arange(GSPAN, dtype=jnp.int32), 0))
    prefix_pos = quarter * block_len + jnp.arange(block_len, dtype=jnp.int32)
    stored_keys = rope(
        prefix_kv[:, 0].reshape(block_len, kv_heads, head_dim).astype(jnp.float32), prefix_pos
    ).astype(jnp.bfloat16)
    stored_values = prefix_kv[:, 1].reshape(block_len, kv_heads, head_dim)

    z_bit = az_index % 2
    core_other = swap_with_partner(grouped_queries, "rc", n_rc)
    pair = jnp.where(
        rc_index == 0,
        jnp.stack([grouped_queries, core_other]),
        jnp.stack([core_other, grouped_queries]),
    )
    z_other = swap_with_partner(pair, "az", n_az)
    group_queries = jnp.where(
        z_bit == 0, jnp.concatenate([pair, z_other]), jnp.concatenate([z_other, pair])
    )
    runs = group_queries.shape[0]
    states = partial_attention(
        group_queries.reshape(runs * slots_here, kv_heads, group, head_dim),
        stored_keys,
        stored_values,
        None,
    )
    states = states.reshape(kv_heads, group, runs, slots_here, head_dim + 2)
    keep = lax.dynamic_slice_in_dim(states, z_bit * 2, 2, 2)
    send = lax.dynamic_slice_in_dim(states, (1 - z_bit) * 2, 2, 2)
    states = combine_states(keep, swap_with_partner(send, "az", n_az))
    keep = lax.dynamic_slice_in_dim(states, rc_index, 1, 2)
    send = lax.dynamic_slice_in_dim(states, 1 - rc_index, 1, 2)
    prefix_state = combine_states(keep, swap_with_partner(send, "rc", n_rc))[:, :, 0]

    slot_ids = jnp.arange(slots_here, dtype=jnp.int32)
    allowed = (request_of[:, None] == request_of[None, :]) & (
        slot_ids[None, :] <= slot_ids[:, None]
    )
    suffix_state = partial_attention(grouped_queries, key_rows, value_rows, allowed)
    merged = combine_states(prefix_state, suffix_state)
    attended = (
        jnp.transpose(merged[..., :head_dim] / merged[..., head_dim + 1 :], (2, 0, 1, 3))
        .reshape(slots_here, q_heads * head_dim)
        .astype(jnp.bfloat16)
    )

    head_terms = jnp.dot(attended, w_out, preferred_element_type=jnp.float32)
    rows_here = slots_here // n_mlp
    head_rows = lax.dynamic_slice_in_dim(head_terms, mlp_index * rows_here, rows_here, 0)
    for shift in range(1, n_mlp):
        target = (mlp_index + shift) % n_mlp
        outgoing = lax.dynamic_slice_in_dim(head_terms, target * rows_here, rows_here, 0)
        incoming = shifted(outgoing.astype(jnp.bfloat16), "mlp", n_mlp, shift)
        head_rows = head_rows + incoming.astype(jnp.float32)
    row_start = mlp_index * rows_here
    hidden_rows = lax.dynamic_slice_in_dim(hidden_f, row_start, rows_here, 0)
    live_rows = lax.dynamic_slice_in_dim(live, row_start, rows_here, 0)
    residual = (hidden_rows + head_rows).astype(jnp.bfloat16)
    normed_mlp = rms_norm(residual.astype(jnp.float32), mlp_gain).astype(jnp.bfloat16)

    n_ax = lax.axis_size("ax")
    tokens = gather_plane(normed_mlp, n_ax, n_az)
    tokens_ring = jnp.concatenate(
        [
            lax.dynamic_slice_in_dim(tokens, quarter_of[ring] * width_part, width_part, 1)
            for ring in range(n_mlp)
        ],
        axis=1,
    )
    acts = []
    for core in range(n_rc):
        weights_here = gate_up_pair[core].reshape(n_mlp * width_part, 2 * unit_count)
        gate_up = jnp.dot(tokens_ring, weights_here, preferred_element_type=jnp.float32)
        gate = gate_up[:, :unit_count]
        up_part = gate_up[:, unit_count:]
        acts.append((jax.nn.silu(gate) * up_part).astype(jnp.bfloat16))
    down_sum = None
    for core in range(n_rc):
        term = jnp.dot(acts[core], down_pair[core], preferred_element_type=jnp.float32)
        term = term.astype(jnp.bfloat16).astype(jnp.float32)
        down_sum = term if down_sum is None else down_sum + term
    down = reduce_plane(down_sum.astype(jnp.bfloat16), n_ax, n_az)
    down = down.reshape(rows_here, n_mlp, width_part)
    natural = jnp.stack([(mlp_index - j) % n_mlp for j in range(n_mlp)])
    down = jnp.take(down, natural, axis=1).reshape(rows_here, n_mlp * width_part)
    down = down.astype(jnp.float32)
    out_rows = jnp.where(
        live_rows[:, None], residual.astype(jnp.float32) + down, 0.0
    ).astype(jnp.bfloat16)
    arrived = [lax.dynamic_slice_in_dim(out_rows, mlp_index * width_part, width_part, 1)]
    for shift in range(1, n_mlp):
        target = (mlp_index + shift) % n_mlp
        outgoing = lax.dynamic_slice_in_dim(out_rows, target * width_part, width_part, 1)
        arrived.append(shifted(outgoing, "mlp", n_mlp, shift))
    arrived = jnp.stack(arrived)
    shift_of = jnp.stack([(mlp_index - j) % n_mlp for j in range(n_mlp)])
    hidden_out = jnp.take(arrived, shift_of, axis=0).reshape(slots_here, width_part)

    stacked_kv = jnp.stack(
        [
            key_rows.reshape(slots_here, kv_heads * head_dim),
            value_rows.reshape(slots_here, kv_heads * head_dim),
        ],
        axis=1,
    )
    suffix_kv = jnp.where(live[:, None, None], stacked_kv, jnp.zeros_like(stacked_kv))
    return (hidden_out, suffix_kv)


def solution(mesh):
    req_size, mlp_size = mesh.devices.shape
    x_size = req_size // 8
    view = Mesh(
        np.asarray(mesh.devices).reshape(x_size, 4, 2, mlp_size), ("ax", "az", "rc", "mlp")
    )
    placed = (
        P(REQ, None),
        P(),
        P(None, "mlp"),
        P(None, "mlp"),
        P(None, "mlp"),
        P("mlp", None),
        P(),
        P("mlp", REQ),
        P("mlp", REQ),
        P(REQ, "mlp"),
        P(REQ, None, "mlp"),
        P(REQ, None),
        P(),
    )
    return jax.shard_map(
        layer,
        mesh=view,
        in_specs=placed,
        out_specs=(P(REQ, "mlp"), P(REQ, None, "mlp")),
        check_vma=False,
    )
```

```python
import math

import jax
import jax.numpy as jnp
import numpy as np
from jax import lax
from jax.experimental import pallas as pl
from jax.sharding import Mesh
from jax.sharding import PartitionSpec as P


HEAD_DIM = 128
PREFIX = 8192
GSPAN = 4

REQ = ("ax", "az", "rc")

rope_base = 500000.0
eps = 1e-05


def shifted(value, axis, size, shift):
    return lax.ppermute(value, axis, [(i, (i + shift) % size) for i in range(size)])


def gather_plane(rows, n_ax, n_az):
    half = rows.shape[1] // 2
    part_a = rows[:, :half]
    part_b = rows[:, half:]
    a_z = jnp.stack([part_a] + [shifted(part_a, "az", n_az, d) for d in range(1, n_az)])
    b_x = jnp.stack([part_b] + [shifted(part_b, "ax", n_ax, d) for d in range(1, n_ax)])
    a_zx = jnp.stack([a_z] + [shifted(a_z, "ax", n_ax, d) for d in range(1, n_ax)])
    b_xz = jnp.stack([b_x] + [shifted(b_x, "az", n_az, d) for d in range(1, n_az)])
    return jnp.concatenate(
        [a_zx.reshape(-1, half), jnp.swapaxes(b_xz, 0, 1).reshape(-1, half)], axis=1
    )


def reduce_plane(blocks, n_ax, n_az):
    rows = blocks.shape[0] // (n_ax * n_az)
    half = blocks.shape[1] // 2
    blocks = blocks.reshape(n_ax, n_az, rows, 2 * half)
    part_a = blocks[..., :half]
    part_b = blocks[..., half:]

    def fold(stack, axis, size):
        total = stack[0].astype(jnp.float32)
        for d in range(1, size):
            total = total + shifted(stack[d], axis, size, -d).astype(jnp.float32)
        return total

    a_1 = fold(part_a, "ax", n_ax).astype(jnp.bfloat16)
    a_2 = fold(a_1, "az", n_az)
    b_1 = fold(jnp.swapaxes(part_b, 0, 1), "az", n_az).astype(jnp.bfloat16)
    b_2 = fold(b_1, "ax", n_ax)
    return jnp.concatenate([a_2, b_2], axis=1)


def swap_with_partner(value, axis, size):
    return lax.ppermute(value, axis, [(source, source ^ 1) for source in range(size)])


def rope(values, positions):
    half = values.shape[-1] // 2
    freq = rope_base ** (-jnp.arange(half, dtype=jnp.float32) * 2.0 / values.shape[-1])
    angle = positions.astype(jnp.float32)[:, None] * freq[None, :]
    cosine = jnp.cos(angle)[:, None, :]
    sine = jnp.sin(angle)[:, None, :]
    former = values[..., :half]
    latter = values[..., half:]
    return jnp.concatenate(
        [former * cosine - latter * sine, latter * cosine + former * sine], axis=-1
    )


def rms_norm(values, gain):
    return (
        values
        * lax.rsqrt(jnp.mean(values * values, axis=-1, keepdims=True) + eps)
        * gain.astype(jnp.float32)
    )


def slot_layout(lengths, slot_count):
    ends = jnp.cumsum(lengths)
    starts = ends - lengths
    slot_ids = jnp.arange(slot_count, dtype=jnp.int32)
    request_of = jnp.sum((slot_ids[:, None] >= ends[None, :]).astype(jnp.int32), axis=1)
    picks = (request_of[:, None] == jnp.arange(lengths.shape[0], dtype=jnp.int32)[None, :]).astype(
        jnp.int32
    )
    start_of = jnp.sum(picks * starts[None, :], axis=1)
    positions = PREFIX + slot_ids - start_of
    return (request_of, request_of < lengths.shape[0], positions)


def partial_attention(grouped_queries, key_block, value_block, allowed):
    scores = jnp.einsum(
        "qkgd,nkd->kgqn", grouped_queries, key_block, preferred_element_type=jnp.float32
    ) / math.sqrt(grouped_queries.shape[-1])
    if allowed is not None:
        scores = jnp.where(allowed[None, None], scores, -jnp.inf)
    peak = jnp.max(scores, axis=-1)
    weights = jnp.exp(scores - peak[..., None])
    weight_sum = jnp.sum(weights, axis=-1)
    summed = jnp.einsum(
        "kgqn,nkd->kgqd",
        weights.astype(jnp.bfloat16),
        value_block,
        preferred_element_type=jnp.float32,
    )
    return jnp.concatenate([summed, peak[..., None], weight_sum[..., None]], axis=-1)


def block_attention_kernel(q_ref, k_ref, v_ref, o_ref):
    head_dim = q_ref.shape[-1]
    scores = lax.dot_general(
        q_ref[...], k_ref[...], (((1,), (1,)), ((), ())), preferred_element_type=jnp.float32
    ) / math.sqrt(head_dim)
    peak = jnp.max(scores, axis=1, keepdims=True)
    weights = jnp.exp(scores - peak)
    o_ref[:, :head_dim] = jnp.dot(
        weights.astype(jnp.bfloat16), v_ref[...], preferred_element_type=jnp.float32
    )
    o_ref[:, head_dim : head_dim + 1] = peak
    o_ref[:, head_dim + 1 : head_dim + 2] = jnp.sum(weights, axis=1, keepdims=True)


def block_attention(queries, keys, values, tile=256):
    rows, head_dim = queries.shape
    count = keys.shape[0]
    return pl.pallas_call(
        block_attention_kernel,
        grid=(rows // tile,),
        in_specs=[
            pl.BlockSpec((tile, head_dim), lambda i: (i, 0)),
            pl.BlockSpec((count, head_dim), lambda i: (0, 0)),
            pl.BlockSpec((count, head_dim), lambda i: (0, 0)),
        ],
        out_specs=pl.BlockSpec((tile, head_dim + 2), lambda i: (i, 0)),
        out_shape=jax.ShapeDtypeStruct((rows, head_dim + 2), jnp.float32),
        cost_estimate=pl.CostEstimate(
            flops=4 * rows * count * head_dim,
            transcendentals=rows * count,
            bytes_accessed=2 * (rows + 2 * count) * head_dim + 4 * rows * (head_dim + 2),
        ),
    )(queries, keys, values)


def combine_states(former, latter):
    head_dim = former.shape[-1] - 2
    peak = jnp.maximum(former[..., head_dim], latter[..., head_dim])
    scale_former = jnp.exp(former[..., head_dim] - peak)
    scale_latter = jnp.exp(latter[..., head_dim] - peak)
    summed = (
        former[..., :head_dim] * scale_former[..., None]
        + latter[..., :head_dim] * scale_latter[..., None]
    )
    weight_sum = (
        former[..., head_dim + 1] * scale_former + latter[..., head_dim + 1] * scale_latter
    )
    return jnp.concatenate([summed, peak[..., None], weight_sum[..., None]], axis=-1)


def layer(
    hidden_in,
    attn_gain,
    w_query,
    w_key,
    w_value,
    w_out,
    mlp_gain,
    w_gate,
    w_up,
    w_down,
    prefix_kv,
    suffix_lengths,
    prefix_owner,
):
    slots_here = hidden_in.shape[0]
    head_dim = HEAD_DIM
    kv_heads = w_key.shape[1] // head_dim
    q_heads = w_query.shape[1] // head_dim
    group = q_heads // kv_heads
    block_len = prefix_kv.shape[0]
    unit_count = w_gate.shape[1]
    width_part = w_gate.shape[0]
    n_az = lax.axis_size("az")
    n_rc = lax.axis_size("rc")
    n_mlp = lax.axis_size("mlp")
    az_index = lax.axis_index("az")
    rc_index = lax.axis_index("rc")
    req_index = (lax.axis_index("ax") * n_az + az_index) * n_rc + rc_index
    mlp_index = lax.axis_index("mlp")

    own = (jnp.concatenate([w_gate, w_up], axis=1), w_down)
    from_left = lax.ppermute(own, "mlp", [(i, (i + 1) % n_mlp) for i in range(n_mlp)])
    from_right = lax.ppermute(own, "mlp", [(i, (i - 1) % n_mlp) for i in range(n_mlp)])
    half_gu = width_part // 2
    half_wd = unit_count // 2
    relay_a = lax.ppermute(
        (from_left[0][:half_gu], from_left[1][:half_wd]),
        "mlp",
        [(i, (i + 1) % n_mlp) for i in range(n_mlp)],
    )
    relay_b = lax.ppermute(
        (from_right[0][half_gu:], from_right[1][half_wd:]),
        "mlp",
        [(i, (i - 1) % n_mlp) for i in range(n_mlp)],
    )
    across = (
        jnp.concatenate([relay_a[0], relay_b[0]], axis=0),
        jnp.concatenate([relay_a[1], relay_b[1]], axis=0),
    )
    gate_up_ring = jnp.stack([own[0], from_left[0], across[0], from_right[0]])
    down_ring = jnp.stack([own[1], from_left[1], across[1], from_right[1]], axis=1)
    down_ring = down_ring.reshape(unit_count, n_mlp * width_part)
    gate_up_other, down_other = swap_with_partner((gate_up_ring, down_ring), "rc", n_rc)
    gate_up_pair = (gate_up_ring, gate_up_other)
    down_pair = (down_ring, down_other)
    quarter_of = [(mlp_index - ring) % n_mlp for ring in range(n_mlp)]

    request_of, live, positions = slot_layout(suffix_lengths[0], slots_here)
    hidden_f = hidden_in.astype(jnp.float32)
    normed = rms_norm(hidden_f, attn_gain).astype(jnp.bfloat16)
    query_rows = rope(
        jnp.dot(normed, w_query, preferred_element_type=jnp.float32).reshape(
            slots_here, q_heads, head_dim
        ),
        positions,
    ).astype(jnp.bfloat16)
    key_rows = rope(
        jnp.dot(normed, w_key, preferred_element_type=jnp.float32).reshape(
            slots_here, kv_heads, head_dim
        ),
        positions,
    ).astype(jnp.bfloat16)
    value_rows = (
        jnp.dot(normed, w_value, preferred_element_type=jnp.float32)
        .astype(jnp.bfloat16)
        .reshape(slots_here, kv_heads, head_dim)
    )
    grouped_queries = query_rows.reshape(slots_here, kv_heads, group, head_dim)

    place = req_index % GSPAN
    group_id = req_index // GSPAN
    owners = lax.dynamic_index_in_dim(prefix_owner, group_id, 0, keepdims=False)
    quarter = jnp.sum(jnp.where(owners == place, jnp.arange(GSPAN, dtype=jnp.int32), 0))
    prefix_pos = quarter * block_len + jnp.arange(block_len, dtype=jnp.int32)
    stored_keys = rope(
        prefix_kv[:, 0].reshape(block_len, kv_heads, head_dim).astype(jnp.float32), prefix_pos
    ).astype(jnp.bfloat16)
    stored_values = prefix_kv[:, 1].reshape(block_len, kv_heads, head_dim)

    core_other = swap_with_partner(grouped_queries, "rc", n_rc)
    pair = jnp.stack([grouped_queries, core_other])
    z_other = swap_with_partner(pair, "az", n_az)
    group_queries = jnp.concatenate([pair, z_other])
    runs = group_queries.shape[0]
    rows_in = jnp.transpose(
        group_queries.reshape(runs * slots_here, kv_heads, group, head_dim), (1, 2, 0, 3)
    )
    states = block_attention(
        rows_in.reshape(kv_heads * group * runs * slots_here, head_dim),
        stored_keys.reshape(block_len, head_dim),
        stored_values.reshape(block_len, head_dim),
    )
    states = states.reshape(kv_heads, group, runs, slots_here, head_dim + 2)
    states = combine_states(states[:, :, :2], swap_with_partner(states[:, :, 2:], "az", n_az))
    prefix_state = combine_states(states[:, :, 0], swap_with_partner(states[:, :, 1], "rc", n_rc))

    slot_ids = jnp.arange(slots_here, dtype=jnp.int32)
    allowed = (request_of[:, None] == request_of[None, :]) & (
        slot_ids[None, :] <= slot_ids[:, None]
    )
    suffix_state = partial_attention(grouped_queries, key_rows, value_rows, allowed)
    merged = combine_states(prefix_state, suffix_state)
    attended = (
        jnp.transpose(merged[..., :head_dim] / merged[..., head_dim + 1 :], (2, 0, 1, 3))
        .reshape(slots_here, q_heads * head_dim)
        .astype(jnp.bfloat16)
    )

    head_terms = jnp.dot(attended, w_out, preferred_element_type=jnp.float32)
    rows_here = slots_here // n_mlp
    head_rows = lax.dynamic_slice_in_dim(head_terms, mlp_index * rows_here, rows_here, 0)
    for shift in range(1, n_mlp):
        target = (mlp_index + shift) % n_mlp
        outgoing = lax.dynamic_slice_in_dim(head_terms, target * rows_here, rows_here, 0)
        incoming = shifted(outgoing.astype(jnp.bfloat16), "mlp", n_mlp, shift)
        head_rows = head_rows + incoming.astype(jnp.float32)
    row_start = mlp_index * rows_here
    hidden_rows = lax.dynamic_slice_in_dim(hidden_f, row_start, rows_here, 0)
    live_rows = lax.dynamic_slice_in_dim(live, row_start, rows_here, 0)
    residual = (hidden_rows + head_rows).astype(jnp.bfloat16)
    normed_mlp = rms_norm(residual.astype(jnp.float32), mlp_gain).astype(jnp.bfloat16)

    n_ax = lax.axis_size("ax")
    tokens = gather_plane(normed_mlp, n_ax, n_az)
    tokens_ring = jnp.concatenate(
        [
            lax.dynamic_slice_in_dim(tokens, quarter_of[ring] * width_part, width_part, 1)
            for ring in range(n_mlp)
        ],
        axis=1,
    )
    acts = []
    for core in range(n_rc):
        weights_here = gate_up_pair[core].reshape(n_mlp * width_part, 2 * unit_count)
        gate_up = jnp.dot(tokens_ring, weights_here, preferred_element_type=jnp.float32)
        gate = gate_up[:, :unit_count]
        up_part = gate_up[:, unit_count:]
        acts.append((jax.nn.silu(gate) * up_part).astype(jnp.bfloat16))
    down_sum = None
    for core in range(n_rc):
        term = jnp.dot(acts[core], down_pair[core], preferred_element_type=jnp.float32)
        term = term.astype(jnp.bfloat16).astype(jnp.float32)
        down_sum = term if down_sum is None else down_sum + term
    down = reduce_plane(down_sum.astype(jnp.bfloat16), n_ax, n_az)
    down = down.reshape(rows_here, n_mlp, width_part)
    natural = jnp.stack([(mlp_index - j) % n_mlp for j in range(n_mlp)])
    down = jnp.take(down, natural, axis=1).reshape(rows_here, n_mlp * width_part)
    down = down.astype(jnp.float32)
    out_rows = jnp.where(
        live_rows[:, None], residual.astype(jnp.float32) + down, 0.0
    ).astype(jnp.bfloat16)
    arrived = [lax.dynamic_slice_in_dim(out_rows, mlp_index * width_part, width_part, 1)]
    for shift in range(1, n_mlp):
        target = (mlp_index + shift) % n_mlp
        outgoing = lax.dynamic_slice_in_dim(out_rows, target * width_part, width_part, 1)
        arrived.append(shifted(outgoing, "mlp", n_mlp, shift))
    arrived = jnp.stack(arrived)
    shift_of = jnp.stack([(mlp_index - j) % n_mlp for j in range(n_mlp)])
    hidden_out = jnp.take(arrived, shift_of, axis=0).reshape(slots_here, width_part)

    stacked_kv = jnp.stack(
        [
            key_rows.reshape(slots_here, kv_heads * head_dim),
            value_rows.reshape(slots_here, kv_heads * head_dim),
        ],
        axis=1,
    )
    suffix_kv = jnp.where(live[:, None, None], stacked_kv, jnp.zeros_like(stacked_kv))
    return (hidden_out, suffix_kv)


def solution(mesh):
    req_size, mlp_size = mesh.devices.shape
    x_size = req_size // 8
    view = Mesh(
        np.asarray(mesh.devices).reshape(x_size, 4, 2, mlp_size), ("ax", "az", "rc", "mlp")
    )
    placed = (
        P(REQ, None),
        P(),
        P(None, "mlp"),
        P(None, "mlp"),
        P(None, "mlp"),
        P("mlp", None),
        P(),
        P("mlp", REQ),
        P("mlp", REQ),
        P(REQ, "mlp"),
        P(REQ, None, "mlp"),
        P(REQ, None),
        P(),
    )
    return jax.shard_map(
        layer,
        mesh=view,
        in_specs=placed,
        out_specs=(P(REQ, "mlp"), P(REQ, None, "mlp")),
        check_vma=False,
    )
```

```python
import math

import jax
import jax.numpy as jnp
import numpy as np
from jax import lax
from jax.experimental import pallas as pl
from jax.sharding import Mesh
from jax.sharding import PartitionSpec as P


HEAD_DIM = 128
PREFIX = 8192
GSPAN = 4

REQ = ("ax", "az", "rc")

rope_base = 500000.0
eps = 1e-05


def shifted(value, axis, size, shift):
    return lax.ppermute(value, axis, [(i, (i + shift) % size) for i in range(size)])


def gather_plane(rows, n_ax, n_az):
    half = rows.shape[1] // 2
    part_a = rows[:, :half]
    part_b = rows[:, half:]
    a_z = jnp.stack([part_a] + [shifted(part_a, "az", n_az, d) for d in range(1, n_az)])
    b_x = jnp.stack([part_b] + [shifted(part_b, "ax", n_ax, d) for d in range(1, n_ax)])
    a_zx = jnp.stack([a_z] + [shifted(a_z, "ax", n_ax, d) for d in range(1, n_ax)])
    b_xz = jnp.stack([b_x] + [shifted(b_x, "az", n_az, d) for d in range(1, n_az)])
    return jnp.concatenate(
        [a_zx.reshape(-1, half), jnp.swapaxes(b_xz, 0, 1).reshape(-1, half)], axis=1
    )


def reduce_plane(blocks, n_ax, n_az):
    rows = blocks.shape[0] // (n_ax * n_az)
    half = blocks.shape[1] // 2
    blocks = blocks.reshape(n_ax, n_az, rows, 2 * half)
    part_a = blocks[..., :half]
    part_b = blocks[..., half:]

    def fold(stack, axis, size):
        total = stack[0].astype(jnp.float32)
        for d in range(1, size):
            total = total + shifted(stack[d], axis, size, -d).astype(jnp.float32)
        return total

    a_1 = fold(part_a, "ax", n_ax).astype(jnp.bfloat16)
    a_2 = fold(a_1, "az", n_az)
    b_1 = fold(jnp.swapaxes(part_b, 0, 1), "az", n_az).astype(jnp.bfloat16)
    b_2 = fold(b_1, "ax", n_ax)
    return jnp.concatenate([a_2, b_2], axis=1)


def swap_with_partner(value, axis, size):
    return lax.ppermute(value, axis, [(source, source ^ 1) for source in range(size)])


def rope(values, positions):
    half = values.shape[-1] // 2
    freq = rope_base ** (-jnp.arange(half, dtype=jnp.float32) * 2.0 / values.shape[-1])
    angle = positions.astype(jnp.float32)[:, None] * freq[None, :]
    cosine = jnp.cos(angle)[:, None, :]
    sine = jnp.sin(angle)[:, None, :]
    former = values[..., :half]
    latter = values[..., half:]
    return jnp.concatenate(
        [former * cosine - latter * sine, latter * cosine + former * sine], axis=-1
    )


def rms_norm(values, gain):
    return (
        values
        * lax.rsqrt(jnp.mean(values * values, axis=-1, keepdims=True) + eps)
        * gain.astype(jnp.float32)
    )


def slot_layout(lengths, slot_count):
    ends = jnp.cumsum(lengths)
    starts = ends - lengths
    slot_ids = jnp.arange(slot_count, dtype=jnp.int32)
    request_of = jnp.sum((slot_ids[:, None] >= ends[None, :]).astype(jnp.int32), axis=1)
    picks = (request_of[:, None] == jnp.arange(lengths.shape[0], dtype=jnp.int32)[None, :]).astype(
        jnp.int32
    )
    start_of = jnp.sum(picks * starts[None, :], axis=1)
    positions = PREFIX + slot_ids - start_of
    return (request_of, request_of < lengths.shape[0], positions)


def partial_attention(grouped_queries, key_block, value_block, allowed):
    scores = jnp.einsum(
        "qkgd,nkd->kgqn", grouped_queries, key_block, preferred_element_type=jnp.float32
    ) / math.sqrt(grouped_queries.shape[-1])
    if allowed is not None:
        scores = jnp.where(allowed[None, None], scores, -jnp.inf)
    peak = jnp.max(scores, axis=-1)
    weights = jnp.exp(scores - peak[..., None])
    weight_sum = jnp.sum(weights, axis=-1)
    summed = jnp.einsum(
        "kgqn,nkd->kgqd",
        weights.astype(jnp.bfloat16),
        value_block,
        preferred_element_type=jnp.float32,
    )
    return jnp.concatenate([summed, peak[..., None], weight_sum[..., None]], axis=-1)


def block_attention_kernel(q_ref, k_ref, v_ref, o_ref, m_ref, l_ref):
    scores = lax.dot_general(
        q_ref[...], k_ref[...], (((1,), (1,)), ((), ())), preferred_element_type=jnp.float32
    ) / math.sqrt(q_ref.shape[-1])
    peak = jnp.max(scores, axis=1, keepdims=True)
    weights = jnp.exp(scores - peak)
    m_ref[...] = peak
    l_ref[...] = jnp.sum(weights, axis=1, keepdims=True)
    o_ref[...] = jnp.dot(
        weights.astype(jnp.bfloat16), v_ref[...], preferred_element_type=jnp.float32
    )


def block_attention(queries, keys, values, tile=128):
    rows, head_dim = queries.shape
    count = keys.shape[0]
    summed, peak, weight_sum = pl.pallas_call(
        block_attention_kernel,
        grid=(rows // tile,),
        in_specs=[
            pl.BlockSpec((tile, head_dim), lambda i: (i, 0)),
            pl.BlockSpec((count, head_dim), lambda i: (0, 0)),
            pl.BlockSpec((count, head_dim), lambda i: (0, 0)),
        ],
        out_specs=[
            pl.BlockSpec((tile, head_dim), lambda i: (i, 0)),
            pl.BlockSpec((tile, 1), lambda i: (i, 0)),
            pl.BlockSpec((tile, 1), lambda i: (i, 0)),
        ],
        out_shape=[
            jax.ShapeDtypeStruct((rows, head_dim), jnp.float32),
            jax.ShapeDtypeStruct((rows, 1), jnp.float32),
            jax.ShapeDtypeStruct((rows, 1), jnp.float32),
        ],
        cost_estimate=pl.CostEstimate(
            flops=4 * rows * count * head_dim,
            transcendentals=rows * count,
            bytes_accessed=2 * (rows + 2 * count) * head_dim + 4 * rows * (head_dim + 2),
        ),
    )(queries, keys, values)
    return jnp.concatenate([summed, peak, weight_sum], axis=-1)


def combine_states(former, latter):
    head_dim = former.shape[-1] - 2
    peak = jnp.maximum(former[..., head_dim], latter[..., head_dim])
    scale_former = jnp.exp(former[..., head_dim] - peak)
    scale_latter = jnp.exp(latter[..., head_dim] - peak)
    summed = (
        former[..., :head_dim] * scale_former[..., None]
        + latter[..., :head_dim] * scale_latter[..., None]
    )
    weight_sum = (
        former[..., head_dim + 1] * scale_former + latter[..., head_dim + 1] * scale_latter
    )
    return jnp.concatenate([summed, peak[..., None], weight_sum[..., None]], axis=-1)


def layer(
    hidden_in,
    attn_gain,
    w_query,
    w_key,
    w_value,
    w_out,
    mlp_gain,
    w_gate,
    w_up,
    w_down,
    prefix_kv,
    suffix_lengths,
    prefix_owner,
):
    slots_here = hidden_in.shape[0]
    head_dim = HEAD_DIM
    kv_heads = w_key.shape[1] // head_dim
    q_heads = w_query.shape[1] // head_dim
    group = q_heads // kv_heads
    block_len = prefix_kv.shape[0]
    unit_count = w_gate.shape[1]
    width_part = w_gate.shape[0]
    n_az = lax.axis_size("az")
    n_rc = lax.axis_size("rc")
    n_mlp = lax.axis_size("mlp")
    az_index = lax.axis_index("az")
    rc_index = lax.axis_index("rc")
    req_index = (lax.axis_index("ax") * n_az + az_index) * n_rc + rc_index
    mlp_index = lax.axis_index("mlp")

    own = (jnp.concatenate([w_gate, w_up], axis=1), w_down)
    from_left = lax.ppermute(own, "mlp", [(i, (i + 1) % n_mlp) for i in range(n_mlp)])
    from_right = lax.ppermute(own, "mlp", [(i, (i - 1) % n_mlp) for i in range(n_mlp)])
    half_gu = width_part // 2
    half_wd = unit_count // 2
    relay_a = lax.ppermute(
        (from_left[0][:half_gu], from_left[1][:half_wd]),
        "mlp",
        [(i, (i + 1) % n_mlp) for i in range(n_mlp)],
    )
    relay_b = lax.ppermute(
        (from_right[0][half_gu:], from_right[1][half_wd:]),
        "mlp",
        [(i, (i - 1) % n_mlp) for i in range(n_mlp)],
    )
    across = (
        jnp.concatenate([relay_a[0], relay_b[0]], axis=0),
        jnp.concatenate([relay_a[1], relay_b[1]], axis=0),
    )
    gate_up_ring = jnp.stack([own[0], from_left[0], across[0], from_right[0]])
    down_ring = jnp.stack([own[1], from_left[1], across[1], from_right[1]], axis=1)
    down_ring = down_ring.reshape(unit_count, n_mlp * width_part)
    gate_up_other, down_other = swap_with_partner((gate_up_ring, down_ring), "rc", n_rc)
    gate_up_pair = (gate_up_ring, gate_up_other)
    down_pair = (down_ring, down_other)
    quarter_of = [(mlp_index - ring) % n_mlp for ring in range(n_mlp)]

    request_of, live, positions = slot_layout(suffix_lengths[0], slots_here)
    hidden_f = hidden_in.astype(jnp.float32)
    normed = rms_norm(hidden_f, attn_gain).astype(jnp.bfloat16)
    query_rows = rope(
        jnp.dot(normed, w_query, preferred_element_type=jnp.float32).reshape(
            slots_here, q_heads, head_dim
        ),
        positions,
    ).astype(jnp.bfloat16)
    key_rows = rope(
        jnp.dot(normed, w_key, preferred_element_type=jnp.float32).reshape(
            slots_here, kv_heads, head_dim
        ),
        positions,
    ).astype(jnp.bfloat16)
    value_rows = (
        jnp.dot(normed, w_value, preferred_element_type=jnp.float32)
        .astype(jnp.bfloat16)
        .reshape(slots_here, kv_heads, head_dim)
    )
    grouped_queries = query_rows.reshape(slots_here, kv_heads, group, head_dim)

    place = req_index % GSPAN
    group_id = req_index // GSPAN
    owners = lax.dynamic_index_in_dim(prefix_owner, group_id, 0, keepdims=False)
    quarter = jnp.sum(jnp.where(owners == place, jnp.arange(GSPAN, dtype=jnp.int32), 0))
    prefix_pos = quarter * block_len + jnp.arange(block_len, dtype=jnp.int32)
    stored_keys = rope(
        prefix_kv[:, 0].reshape(block_len, kv_heads, head_dim).astype(jnp.float32), prefix_pos
    ).astype(jnp.bfloat16)
    stored_values = prefix_kv[:, 1].reshape(block_len, kv_heads, head_dim)

    z_bit = az_index % 2
    core_other = swap_with_partner(grouped_queries, "rc", n_rc)
    pair = jnp.where(
        rc_index == 0,
        jnp.stack([grouped_queries, core_other]),
        jnp.stack([core_other, grouped_queries]),
    )
    z_other = swap_with_partner(pair, "az", n_az)
    group_queries = jnp.where(
        z_bit == 0, jnp.concatenate([pair, z_other]), jnp.concatenate([z_other, pair])
    )
    runs = group_queries.shape[0]
    rows_in = jnp.transpose(
        group_queries.reshape(runs * slots_here, kv_heads, group, head_dim), (1, 2, 0, 3)
    )
    states = block_attention(
        rows_in.reshape(kv_heads * group * runs * slots_here, head_dim),
        stored_keys.reshape(block_len, head_dim),
        stored_values.reshape(block_len, head_dim),
    )
    states = states.reshape(kv_heads, group, runs, slots_here, head_dim + 2)
    keep = lax.dynamic_slice_in_dim(states, z_bit * 2, 2, 2)
    send = lax.dynamic_slice_in_dim(states, (1 - z_bit) * 2, 2, 2)
    states = combine_states(keep, swap_with_partner(send, "az", n_az))
    keep = lax.dynamic_slice_in_dim(states, rc_index, 1, 2)
    send = lax.dynamic_slice_in_dim(states, 1 - rc_index, 1, 2)
    prefix_state = combine_states(keep, swap_with_partner(send, "rc", n_rc))[:, :, 0]

    slot_ids = jnp.arange(slots_here, dtype=jnp.int32)
    allowed = (request_of[:, None] == request_of[None, :]) & (
        slot_ids[None, :] <= slot_ids[:, None]
    )
    suffix_state = partial_attention(grouped_queries, key_rows, value_rows, allowed)
    merged = combine_states(prefix_state, suffix_state)
    attended = (
        jnp.transpose(merged[..., :head_dim] / merged[..., head_dim + 1 :], (2, 0, 1, 3))
        .reshape(slots_here, q_heads * head_dim)
        .astype(jnp.bfloat16)
    )

    head_terms = jnp.dot(attended, w_out, preferred_element_type=jnp.float32)
    rows_here = slots_here // n_mlp
    head_rows = lax.dynamic_slice_in_dim(head_terms, mlp_index * rows_here, rows_here, 0)
    for shift in range(1, n_mlp):
        target = (mlp_index + shift) % n_mlp
        outgoing = lax.dynamic_slice_in_dim(head_terms, target * rows_here, rows_here, 0)
        incoming = shifted(outgoing.astype(jnp.bfloat16), "mlp", n_mlp, shift)
        head_rows = head_rows + incoming.astype(jnp.float32)
    row_start = mlp_index * rows_here
    hidden_rows = lax.dynamic_slice_in_dim(hidden_f, row_start, rows_here, 0)
    live_rows = lax.dynamic_slice_in_dim(live, row_start, rows_here, 0)
    residual = (hidden_rows + head_rows).astype(jnp.bfloat16)
    normed_mlp = rms_norm(residual.astype(jnp.float32), mlp_gain).astype(jnp.bfloat16)

    n_ax = lax.axis_size("ax")
    tokens = gather_plane(normed_mlp, n_ax, n_az)
    tokens_ring = jnp.concatenate(
        [
            lax.dynamic_slice_in_dim(tokens, quarter_of[ring] * width_part, width_part, 1)
            for ring in range(n_mlp)
        ],
        axis=1,
    )
    acts = []
    for core in range(n_rc):
        weights_here = gate_up_pair[core].reshape(n_mlp * width_part, 2 * unit_count)
        gate_up = jnp.dot(tokens_ring, weights_here, preferred_element_type=jnp.float32)
        gate = gate_up[:, :unit_count]
        up_part = gate_up[:, unit_count:]
        acts.append((jax.nn.silu(gate) * up_part).astype(jnp.bfloat16))
    down_sum = None
    for core in range(n_rc):
        term = jnp.dot(acts[core], down_pair[core], preferred_element_type=jnp.float32)
        term = term.astype(jnp.bfloat16).astype(jnp.float32)
        down_sum = term if down_sum is None else down_sum + term
    down = reduce_plane(down_sum.astype(jnp.bfloat16), n_ax, n_az)
    down = down.reshape(rows_here, n_mlp, width_part)
    natural = jnp.stack([(mlp_index - j) % n_mlp for j in range(n_mlp)])
    down = jnp.take(down, natural, axis=1).reshape(rows_here, n_mlp * width_part)
    down = down.astype(jnp.float32)
    out_rows = jnp.where(
        live_rows[:, None], residual.astype(jnp.float32) + down, 0.0
    ).astype(jnp.bfloat16)
    arrived = [lax.dynamic_slice_in_dim(out_rows, mlp_index * width_part, width_part, 1)]
    for shift in range(1, n_mlp):
        target = (mlp_index + shift) % n_mlp
        outgoing = lax.dynamic_slice_in_dim(out_rows, target * width_part, width_part, 1)
        arrived.append(shifted(outgoing, "mlp", n_mlp, shift))
    arrived = jnp.stack(arrived)
    shift_of = jnp.stack([(mlp_index - j) % n_mlp for j in range(n_mlp)])
    hidden_out = jnp.take(arrived, shift_of, axis=0).reshape(slots_here, width_part)

    stacked_kv = jnp.stack(
        [
            key_rows.reshape(slots_here, kv_heads * head_dim),
            value_rows.reshape(slots_here, kv_heads * head_dim),
        ],
        axis=1,
    )
    suffix_kv = jnp.where(live[:, None, None], stacked_kv, jnp.zeros_like(stacked_kv))
    return (hidden_out, suffix_kv)


def solution(mesh):
    req_size, mlp_size = mesh.devices.shape
    x_size = req_size // 8
    view = Mesh(
        np.asarray(mesh.devices).reshape(x_size, 4, 2, mlp_size), ("ax", "az", "rc", "mlp")
    )
    placed = (
        P(REQ, None),
        P(),
        P(None, "mlp"),
        P(None, "mlp"),
        P(None, "mlp"),
        P("mlp", None),
        P(),
        P("mlp", REQ),
        P("mlp", REQ),
        P(REQ, "mlp"),
        P(REQ, None, "mlp"),
        P(REQ, None),
        P(),
    )
    return jax.shard_map(
        layer,
        mesh=view,
        in_specs=placed,
        out_specs=(P(REQ, "mlp"), P(REQ, None, "mlp")),
        check_vma=False,
    )
```

```python
import math

import jax
import jax.numpy as jnp
import numpy as np
from jax import lax
from jax.experimental import pallas as pl
from jax.sharding import Mesh
from jax.sharding import PartitionSpec as P


HEAD_DIM = 128
PREFIX = 8192
GSPAN = 4

REQ = ("ax", "az", "rc")

rope_base = 500000.0
eps = 1e-05


def shifted(value, axis, size, shift):
    return lax.ppermute(value, axis, [(i, (i + shift) % size) for i in range(size)])


def gather_plane(rows, n_ax, n_az):
    half = rows.shape[1] // 2
    part_a = rows[:, :half]
    part_b = rows[:, half:]
    a_z = jnp.stack([part_a] + [shifted(part_a, "az", n_az, d) for d in range(1, n_az)])
    b_x = jnp.stack([part_b] + [shifted(part_b, "ax", n_ax, d) for d in range(1, n_ax)])
    a_zx = jnp.stack([a_z] + [shifted(a_z, "ax", n_ax, d) for d in range(1, n_ax)])
    b_xz = jnp.stack([b_x] + [shifted(b_x, "az", n_az, d) for d in range(1, n_az)])
    return jnp.concatenate(
        [a_zx.reshape(-1, half), jnp.swapaxes(b_xz, 0, 1).reshape(-1, half)], axis=1
    )


def reduce_plane(blocks, n_ax, n_az):
    rows = blocks.shape[0] // (n_ax * n_az)
    half = blocks.shape[1] // 2
    blocks = blocks.reshape(n_ax, n_az, rows, 2 * half)
    part_a = blocks[..., :half]
    part_b = blocks[..., half:]

    def fold(stack, axis, size):
        total = stack[0].astype(jnp.float32)
        for d in range(1, size):
            total = total + shifted(stack[d], axis, size, -d).astype(jnp.float32)
        return total

    a_1 = fold(part_a, "ax", n_ax).astype(jnp.bfloat16)
    a_2 = fold(a_1, "az", n_az)
    b_1 = fold(jnp.swapaxes(part_b, 0, 1), "az", n_az).astype(jnp.bfloat16)
    b_2 = fold(b_1, "ax", n_ax)
    return jnp.concatenate([a_2, b_2], axis=1)


def swap_with_partner(value, axis, size):
    return lax.ppermute(value, axis, [(source, source ^ 1) for source in range(size)])


def rope(values, positions):
    half = values.shape[-1] // 2
    freq = rope_base ** (-jnp.arange(half, dtype=jnp.float32) * 2.0 / values.shape[-1])
    angle = positions.astype(jnp.float32)[:, None] * freq[None, :]
    cosine = jnp.cos(angle)[:, None, :]
    sine = jnp.sin(angle)[:, None, :]
    former = values[..., :half]
    latter = values[..., half:]
    return jnp.concatenate(
        [former * cosine - latter * sine, latter * cosine + former * sine], axis=-1
    )


def rms_norm(values, gain):
    return (
        values
        * lax.rsqrt(jnp.mean(values * values, axis=-1, keepdims=True) + eps)
        * gain.astype(jnp.float32)
    )


def slot_layout(lengths, slot_count):
    ends = jnp.cumsum(lengths)
    starts = ends - lengths
    slot_ids = jnp.arange(slot_count, dtype=jnp.int32)
    request_of = jnp.sum((slot_ids[:, None] >= ends[None, :]).astype(jnp.int32), axis=1)
    picks = (request_of[:, None] == jnp.arange(lengths.shape[0], dtype=jnp.int32)[None, :]).astype(
        jnp.int32
    )
    start_of = jnp.sum(picks * starts[None, :], axis=1)
    positions = PREFIX + slot_ids - start_of
    return (request_of, request_of < lengths.shape[0], positions)


def partial_attention(grouped_queries, key_block, value_block, allowed):
    scores = jnp.einsum(
        "qkgd,nkd->kgqn", grouped_queries, key_block, preferred_element_type=jnp.float32
    ) / math.sqrt(grouped_queries.shape[-1])
    if allowed is not None:
        scores = jnp.where(allowed[None, None], scores, -jnp.inf)
    peak = jnp.max(scores, axis=-1)
    weights = jnp.exp(scores - peak[..., None])
    weight_sum = jnp.sum(weights, axis=-1)
    summed = jnp.einsum(
        "kgqn,nkd->kgqd",
        weights.astype(jnp.bfloat16),
        value_block,
        preferred_element_type=jnp.float32,
    )
    return jnp.concatenate([summed, peak[..., None], weight_sum[..., None]], axis=-1)


def block_attention_kernel(q_ref, k_ref, v_ref, o_ref, m_ref, l_ref):
    scores = lax.dot_general(
        q_ref[...], k_ref[...], (((1,), (1,)), ((), ())), preferred_element_type=jnp.float32
    ) / math.sqrt(q_ref.shape[-1])
    peak = jnp.max(scores, axis=1, keepdims=True)
    weights = jnp.exp(scores - peak)
    m_ref[...] = peak
    l_ref[...] = jnp.sum(weights, axis=1, keepdims=True)
    o_ref[...] = jnp.dot(
        weights.astype(jnp.bfloat16), v_ref[...], preferred_element_type=jnp.float32
    )


def block_attention(queries, keys, values, tile=256):
    rows, head_dim = queries.shape
    count = keys.shape[0]
    summed, peak, weight_sum = pl.pallas_call(
        block_attention_kernel,
        grid=(rows // tile,),
        in_specs=[
            pl.BlockSpec((tile, head_dim), lambda i: (i, 0)),
            pl.BlockSpec((count, head_dim), lambda i: (0, 0)),
            pl.BlockSpec((count, head_dim), lambda i: (0, 0)),
        ],
        out_specs=[
            pl.BlockSpec((tile, head_dim), lambda i: (i, 0)),
            pl.BlockSpec((tile, 1), lambda i: (i, 0)),
            pl.BlockSpec((tile, 1), lambda i: (i, 0)),
        ],
        out_shape=[
            jax.ShapeDtypeStruct((rows, head_dim), jnp.float32),
            jax.ShapeDtypeStruct((rows, 1), jnp.float32),
            jax.ShapeDtypeStruct((rows, 1), jnp.float32),
        ],
        cost_estimate=pl.CostEstimate(
            flops=4 * rows * count * head_dim,
            transcendentals=rows * count,
            bytes_accessed=2 * (rows + 2 * count) * head_dim + 4 * rows * (head_dim + 2),
        ),
    )(queries, keys, values)
    return jnp.concatenate([summed, peak, weight_sum], axis=-1)


def combine_states(former, latter):
    head_dim = former.shape[-1] - 2
    peak = jnp.maximum(former[..., head_dim], latter[..., head_dim])
    scale_former = jnp.exp(former[..., head_dim] - peak)
    scale_latter = jnp.exp(latter[..., head_dim] - peak)
    summed = (
        former[..., :head_dim] * scale_former[..., None]
        + latter[..., :head_dim] * scale_latter[..., None]
    )
    weight_sum = (
        former[..., head_dim + 1] * scale_former + latter[..., head_dim + 1] * scale_latter
    )
    return jnp.concatenate([summed, peak[..., None], weight_sum[..., None]], axis=-1)


def layer(
    hidden_in,
    attn_gain,
    w_query,
    w_key,
    w_value,
    w_out,
    mlp_gain,
    w_gate,
    w_up,
    w_down,
    prefix_kv,
    suffix_lengths,
    prefix_owner,
):
    slots_here = hidden_in.shape[0]
    head_dim = HEAD_DIM
    kv_heads = w_key.shape[1] // head_dim
    q_heads = w_query.shape[1] // head_dim
    group = q_heads // kv_heads
    block_len = prefix_kv.shape[0]
    unit_count = w_gate.shape[1]
    width_part = w_gate.shape[0]
    n_az = lax.axis_size("az")
    n_rc = lax.axis_size("rc")
    n_mlp = lax.axis_size("mlp")
    az_index = lax.axis_index("az")
    rc_index = lax.axis_index("rc")
    req_index = (lax.axis_index("ax") * n_az + az_index) * n_rc + rc_index
    mlp_index = lax.axis_index("mlp")

    own = (jnp.concatenate([w_gate, w_up], axis=1), w_down)
    from_left = lax.ppermute(own, "mlp", [(i, (i + 1) % n_mlp) for i in range(n_mlp)])
    from_right = lax.ppermute(own, "mlp", [(i, (i - 1) % n_mlp) for i in range(n_mlp)])
    half_gu = width_part // 2
    half_wd = unit_count // 2
    relay_a = lax.ppermute(
        (from_left[0][:half_gu], from_left[1][:half_wd]),
        "mlp",
        [(i, (i + 1) % n_mlp) for i in range(n_mlp)],
    )
    relay_b = lax.ppermute(
        (from_right[0][half_gu:], from_right[1][half_wd:]),
        "mlp",
        [(i, (i - 1) % n_mlp) for i in range(n_mlp)],
    )
    across = (
        jnp.concatenate([relay_a[0], relay_b[0]], axis=0),
        jnp.concatenate([relay_a[1], relay_b[1]], axis=0),
    )
    gate_up_ring = jnp.stack([own[0], from_left[0], across[0], from_right[0]])
    down_ring = jnp.stack([own[1], from_left[1], across[1], from_right[1]], axis=1)
    down_ring = down_ring.reshape(unit_count, n_mlp * width_part)
    gate_up_other, down_other = swap_with_partner((gate_up_ring, down_ring), "rc", n_rc)
    gate_up_pair = (gate_up_ring, gate_up_other)
    down_pair = (down_ring, down_other)
    quarter_of = [(mlp_index - ring) % n_mlp for ring in range(n_mlp)]

    request_of, live, positions = slot_layout(suffix_lengths[0], slots_here)
    hidden_f = hidden_in.astype(jnp.float32)
    normed = rms_norm(hidden_f, attn_gain).astype(jnp.bfloat16)
    query_rows = rope(
        jnp.dot(normed, w_query, preferred_element_type=jnp.float32).reshape(
            slots_here, q_heads, head_dim
        ),
        positions,
    ).astype(jnp.bfloat16)
    key_rows = rope(
        jnp.dot(normed, w_key, preferred_element_type=jnp.float32).reshape(
            slots_here, kv_heads, head_dim
        ),
        positions,
    ).astype(jnp.bfloat16)
    value_rows = (
        jnp.dot(normed, w_value, preferred_element_type=jnp.float32)
        .astype(jnp.bfloat16)
        .reshape(slots_here, kv_heads, head_dim)
    )
    grouped_queries = query_rows.reshape(slots_here, kv_heads, group, head_dim)

    place = req_index % GSPAN
    group_id = req_index // GSPAN
    owners = lax.dynamic_index_in_dim(prefix_owner, group_id, 0, keepdims=False)
    quarter = jnp.sum(jnp.where(owners == place, jnp.arange(GSPAN, dtype=jnp.int32), 0))
    prefix_pos = quarter * block_len + jnp.arange(block_len, dtype=jnp.int32)
    stored_keys = rope(
        prefix_kv[:, 0].reshape(block_len, kv_heads, head_dim).astype(jnp.float32), prefix_pos
    ).astype(jnp.bfloat16)
    stored_values = prefix_kv[:, 1].reshape(block_len, kv_heads, head_dim)

    z_bit = az_index % 2
    core_other = swap_with_partner(grouped_queries, "rc", n_rc)
    pair = jnp.where(
        rc_index == 0,
        jnp.stack([grouped_queries, core_other]),
        jnp.stack([core_other, grouped_queries]),
    )
    z_other = swap_with_partner(pair, "az", n_az)
    group_queries = jnp.where(
        z_bit == 0, jnp.concatenate([pair, z_other]), jnp.concatenate([z_other, pair])
    )
    runs = group_queries.shape[0]
    rows_in = jnp.transpose(
        group_queries.reshape(runs * slots_here, kv_heads, group, head_dim), (1, 2, 0, 3)
    )
    states = block_attention(
        rows_in.reshape(kv_heads * group * runs * slots_here, head_dim),
        stored_keys.reshape(block_len, head_dim),
        stored_values.reshape(block_len, head_dim),
    )
    states = states.reshape(kv_heads, group, runs, slots_here, head_dim + 2)
    keep = lax.dynamic_slice_in_dim(states, z_bit * 2, 2, 2)
    send = lax.dynamic_slice_in_dim(states, (1 - z_bit) * 2, 2, 2)
    from_z = swap_with_partner(send, "az", n_az)
    states = combine_states(keep, from_z)
    keep = lax.dynamic_slice_in_dim(states, rc_index, 1, 2)
    send = lax.dynamic_slice_in_dim(states, 1 - rc_index, 1, 2)
    prefix_state = combine_states(keep, swap_with_partner(send, "rc", n_rc))[:, :, 0]

    slot_ids = jnp.arange(slots_here, dtype=jnp.int32)
    allowed = (request_of[:, None] == request_of[None, :]) & (
        slot_ids[None, :] <= slot_ids[:, None]
    )
    suffix_state = partial_attention(grouped_queries, key_rows, value_rows, allowed)
    merged = combine_states(prefix_state, suffix_state)
    attended = (
        jnp.transpose(merged[..., :head_dim] / merged[..., head_dim + 1 :], (2, 0, 1, 3))
        .reshape(slots_here, q_heads * head_dim)
        .astype(jnp.bfloat16)
    )

    head_terms = jnp.dot(attended, w_out, preferred_element_type=jnp.float32)
    rows_here = slots_here // n_mlp
    head_rows = lax.dynamic_slice_in_dim(head_terms, mlp_index * rows_here, rows_here, 0)
    for shift in range(1, n_mlp):
        target = (mlp_index + shift) % n_mlp
        outgoing = lax.dynamic_slice_in_dim(head_terms, target * rows_here, rows_here, 0)
        incoming = shifted(outgoing.astype(jnp.bfloat16), "mlp", n_mlp, shift)
        head_rows = head_rows + incoming.astype(jnp.float32)
    row_start = mlp_index * rows_here
    hidden_rows = lax.dynamic_slice_in_dim(hidden_f, row_start, rows_here, 0)
    live_rows = lax.dynamic_slice_in_dim(live, row_start, rows_here, 0)
    residual = (hidden_rows + head_rows).astype(jnp.bfloat16)
    normed_mlp = rms_norm(residual.astype(jnp.float32), mlp_gain).astype(jnp.bfloat16)

    n_ax = lax.axis_size("ax")
    tokens = gather_plane(normed_mlp, n_ax, n_az)
    tokens_ring = jnp.concatenate(
        [
            lax.dynamic_slice_in_dim(tokens, quarter_of[ring] * width_part, width_part, 1)
            for ring in range(n_mlp)
        ],
        axis=1,
    )
    acts = []
    for core in range(n_rc):
        weights_here = gate_up_pair[core].reshape(n_mlp * width_part, 2 * unit_count)
        gate_up = jnp.dot(tokens_ring, weights_here, preferred_element_type=jnp.float32)
        gate = gate_up[:, :unit_count]
        up_part = gate_up[:, unit_count:]
        acts.append((jax.nn.silu(gate) * up_part).astype(jnp.bfloat16))
    down_sum = None
    for core in range(n_rc):
        term = jnp.dot(acts[core], down_pair[core], preferred_element_type=jnp.float32)
        term = term.astype(jnp.bfloat16).astype(jnp.float32)
        down_sum = term if down_sum is None else down_sum + term
    down = reduce_plane(down_sum.astype(jnp.bfloat16), n_ax, n_az)
    down = down.reshape(rows_here, n_mlp, width_part)
    natural = jnp.stack([(mlp_index - j) % n_mlp for j in range(n_mlp)])
    down = jnp.take(down, natural, axis=1).reshape(rows_here, n_mlp * width_part)
    down = down.astype(jnp.float32)
    out_rows = jnp.where(
        live_rows[:, None], residual.astype(jnp.float32) + down, 0.0
    ).astype(jnp.bfloat16)
    arrived = [lax.dynamic_slice_in_dim(out_rows, mlp_index * width_part, width_part, 1)]
    for shift in range(1, n_mlp):
        target = (mlp_index + shift) % n_mlp
        outgoing = lax.dynamic_slice_in_dim(out_rows, target * width_part, width_part, 1)
        arrived.append(shifted(outgoing, "mlp", n_mlp, shift))
    arrived = jnp.stack(arrived)
    shift_of = jnp.stack([(mlp_index - j) % n_mlp for j in range(n_mlp)])
    hidden_out = jnp.take(arrived, shift_of, axis=0).reshape(slots_here, width_part)

    stacked_kv = jnp.stack(
        [
            key_rows.reshape(slots_here, kv_heads * head_dim),
            value_rows.reshape(slots_here, kv_heads * head_dim),
        ],
        axis=1,
    )
    suffix_kv = jnp.where(live[:, None, None], stacked_kv, jnp.zeros_like(stacked_kv))
    return (hidden_out, suffix_kv)


def solution(mesh):
    req_size, mlp_size = mesh.devices.shape
    x_size = req_size // 8
    view = Mesh(
        np.asarray(mesh.devices).reshape(x_size, 4, 2, mlp_size), ("ax", "az", "rc", "mlp")
    )
    placed = (
        P(REQ, None),
        P(),
        P(None, "mlp"),
        P(None, "mlp"),
        P(None, "mlp"),
        P("mlp", None),
        P(),
        P("mlp", REQ),
        P("mlp", REQ),
        P(REQ, "mlp"),
        P(REQ, None, "mlp"),
        P(REQ, None),
        P(),
    )
    return jax.shard_map(
        layer,
        mesh=view,
        in_specs=placed,
        out_specs=(P(REQ, "mlp"), P(REQ, None, "mlp")),
        check_vma=False,
    )
```
